128 devices in a mesh: dp: 64 (over x, y_lo, z, core), mp: 2 (over y_hi).
Axes of the slice: x: 4, y: 4 (y_hi: 2, y_lo: 2; y = y_hi * 2 + y_lo), z: 4, core: 2. Of those that a mesh axis runs over, the one named last changes fastest.
Arguments:
- tokens: bfloat16 [65536, 1152], P('dp'), may hold values from -8 to 8
- lengths: int32 [1024], P('dp'), may hold values from 1 to 64, as said below
- images: bfloat16 [1024, 1152], P('dp'), may hold values from -12 to 12
- pair_group: int32 [1024], replicated, may hold values from 0 to 511, never falling along the last dimension, each value on 1 to 4 neighbouring positions
- w_up: bfloat16 [1152, 4304], P(None, 'mp'), may hold values from -0.1875 to 0.1875
- w_down: bfloat16 [1152, 4304], P(None, 'mp'), may hold values from -0.09375 to 0.09375
Outputs:
- caption_loss: float32 [1024], P('dp')
- image_grad: float32 [1024, 1152], P('dp')
- up_grad: float32 [1152, 4304], P('dp', 'mp')
- down_grad: float32 [1152, 4304], P('dp', 'mp')
The draws below stay inside these ranges and needn't reach their ends.
Inputs may be any that keep to these rules, and one draw needn't show every extreme that they name: Positions below lengths[c] of caption c are real tokens, the rest padding. `pair_group`: ids never fall along the pairs, and each id is held by 1 to 4 consecutive pairs.
All inputs are finite; a program needn't handle non-finite values.
Results may differ from the reference program's by a relative error of at most 0.0033.
Values may be sent and summed in bfloat16 or wider, within the bound.
No kernel may reach another device: no remote copies, remote signals or barrier semaphores. Data moves between devices by JAX's collectives and lax.ppermute only.
A program may use at most 192 MiB of HBM per device.

```python
import math
import jax
import jax.numpy as jnp
import numpy as np
from jax import lax

D = 1152
FF = 4304
TOKLEN = 64
B_DEV = 16
B_TOTAL = 1024


def draw_lengths(key, part):
    first, second, third = jax.random.split(jax.random.fold_in(key, 11), 3)
    raw = jax.random.randint(first, (B_TOTAL,), 1, TOKLEN + 1)
    spot_long = jax.random.randint(second, (), 0, B_TOTAL)
    offset = jax.random.randint(third, (), 1, B_TOTAL)
    spot_short = (spot_long + offset) % B_TOTAL
    raw = raw.at[spot_long].set(TOKLEN)
    raw = raw.at[spot_short].set(1)
    return raw.astype(jnp.int32)


def caption_direction(key, topic_share):
    base = jax.random.fold_in(key, 101)
    topic_key, index_key, own_key = jax.random.split(base, 3)
    topics = jax.random.normal(topic_key, (16, D), jnp.float32)
    topic_index = jax.random.randint(index_key, (B_TOTAL,), 0, 16)
    chosen = jnp.take(topics, topic_index, axis=0)
    own_part = jax.random.normal(own_key, (B_TOTAL, D), jnp.float32)
    return math.sqrt(topic_share) * chosen + math.sqrt(1.0 - topic_share) * own_part


def draw_tokens(key, part):
    noise_key = jax.random.fold_in(key, 211)
    direction = caption_direction(key, 0.18)
    noise_part = jax.random.normal(noise_key, (B_TOTAL, TOKLEN, D), jnp.float32)
    token_rows = jnp.clip(noise_part + direction[:, None, :], -8.0, 8.0)
    return token_rows.reshape(B_TOTAL * TOKLEN, D).astype(jnp.bfloat16)


def draw_images(key, part):
    noise_key = jax.random.fold_in(key, 307)
    direction = caption_direction(key, 0.18)
    noise_part = jax.random.normal(noise_key, (B_TOTAL, D), jnp.float32)
    image_rows = jnp.clip(direction + noise_part, -12.0, 12.0)
    return image_rows.astype(jnp.bfloat16)


def steps_of(stream_key, shape, cuts, smallest, high):
    def one(dim, blocks):
        heights = jax.random.uniform(jax.random.fold_in(jax.random.fold_in(stream_key, 6), dim), (blocks,), jnp.float32, smallest / len(cuts), high / len(cuts))
        return jnp.repeat(jnp.exp(heights), shape[dim] // blocks).reshape((-1,) + (1,) * (len(shape) - dim - 1))

    factor_of = one(*cuts[0])
    for cut in cuts[1:]:
        factor_of = factor_of * one(*cut)
    return factor_of


def split_up(amount, total, bound, skew):
    loads = [(1 << 20) // math.isqrt(standing ** skew) + 1 for standing in range(2, amount + 1)]
    rest, given = total - bound - (amount - 1), [1] * (amount - 1)
    while rest > 0:
        candidates = [i for i in range(amount - 1) if given[i] < bound]
        whole, remaining = sum([loads[i] for i in candidates]), rest
        for i in candidates:
            addition = min(bound - given[i], max(1, remaining * loads[i] // whole), rest)
            given[i] = given[i] + addition
            rest = rest - addition
    return np.array([bound] + given)


def uneven(key, number_of, total, limit, skew):
    if number_of == 2:
        one = jax.random.randint(key, (), max(1, total - limit), min(limit, total - 1) + 1)
        return jnp.stack([one, total - one])
    sizes = jnp.asarray(split_up(number_of, total, limit, skew), jnp.int32)
    twos = (number_of - 1) // 2
    giver, receiver = sizes[1:1 + 2 * twos:2], sizes[2:2 + 2 * twos:2]
    margin = jnp.minimum(giver - 1, limit - receiver)
    shifted = jax.random.randint(jax.random.fold_in(key, 1), (twos,), 0, 1 << 20) % (margin + 1)
    sizes = sizes.at[1:1 + 2 * twos:2].set(giver - shifted).at[2:2 + 2 * twos:2].set(receiver + shifted)
    return sizes[jax.random.permutation(jax.random.fold_in(key, 2), number_of)]


def centred(key, shape, scale, bound, cuts=(), kind=jnp.bfloat16):
    level = steps_of(key, shape, cuts, -0.22, 0.18) if cuts else 1.0
    array = jax.random.normal(key, shape, jnp.float32) * scale * level
    return jnp.minimum(jnp.maximum(array, -bound), bound).astype(kind)


def setup_inputs(seed: int = 0) -> dict:
    splits = jax.random.split(jax.random.key(seed), 7)
    tokens = draw_tokens(jax.random.fold_in(splits[6], 71), 0)
    lengths = draw_lengths(jax.random.fold_in(splits[6], 71), 0)
    images = draw_images(jax.random.fold_in(splits[6], 71), 0)
    pair_group = jnp.searchsorted(jnp.cumsum(uneven(splits[3], B_TOTAL // 2, B_TOTAL, 4, 0)), jnp.arange(B_TOTAL), side="right").astype(jnp.int32)
    w_up = centred(splits[4], (D, FF), D ** -0.5, 0.1875, ((1, 2),))
    w_down = centred(splits[5], (D, FF), FF ** -0.5, 0.09375, ((1, 2),))
    return {"tokens": tokens, "lengths": lengths, "images": images, "pair_group": pair_group, "w_up": w_up, "w_down": w_down}


LOGIT_SCALE = 117.0
LOGIT_SHIFT = -12.9

def layer_norm(rows):
    center = rows - lax.optimization_barrier(jnp.mean(rows, -1, keepdims=True))
    spread = lax.optimization_barrier(jnp.mean(center * center, -1, keepdims=True))
    return center * lax.rsqrt(spread + 1e-06)

def gelu_pair(pre):
    const = 0.7978845608028654
    inner = const * (pre + 0.044715 * pre * pre * pre)
    tanh_u = jnp.tanh(inner)
    value = 0.5 * pre * (1.0 + tanh_u)
    slope = 0.5 * (1.0 + tanh_u) + 0.5 * pre * (1.0 - tanh_u * tanh_u) * const * (1.0 + 3.0 * 0.044715 * pre * pre)
    return (value, slope)

def front(tok_block, len_block, w_up):
    captions = len_block.shape[0]
    seq_len = tok_block.shape[0] // captions
    tok_float = tok_block.astype(jnp.float32)
    normed = layer_norm(tok_float).astype(jnp.bfloat16)
    pre = jnp.dot(normed, w_up, preferred_element_type=jnp.float32)
    value, slope = gelu_pair(pre)
    position = jnp.arange(seq_len, dtype=jnp.int32)
    valid = (position[None, :] < len_block[:, None]).astype(jnp.float32)
    share = valid / lax.optimization_barrier(jnp.sum(valid, 1, keepdims=True))
    return (normed, value, slope, share, tok_float)

def unit_rows(rows):
    scale = lax.rsqrt(lax.optimization_barrier(jnp.sum(rows * rows, 1, keepdims=True)) + 1e-06)
    return (rows * scale, scale)

def reference(tokens, lengths, images, pair_group, w_up, w_down):
    blocks = B_TOTAL // B_DEV
    tok_blocks = tokens.reshape(blocks, B_DEV * TOKLEN, D)
    len_blocks = lengths.reshape(blocks, B_DEV)

    def forward(pieces):
        tok_block, len_block = pieces
        normed, value, slope, share, tok_float = front(tok_block, len_block, w_up)
        gmean = lax.optimization_barrier(jnp.sum(value.reshape(B_DEV, TOKLEN, FF) * share[:, :, None], 1))
        tmean = lax.optimization_barrier(jnp.sum(tok_float.reshape(B_DEV, TOKLEN, D) * share[:, :, None], 1))
        return (gmean, tmean)
    gmean, tmean = lax.map(forward, (tok_blocks, len_blocks))
    gbar = gmean.reshape(B_TOTAL, FF).astype(jnp.bfloat16)
    tmean = tmean.reshape(B_TOTAL, D)
    pooled = tmean + lax.dot_general(gbar, w_down, (((1,), (1,)), ((), ())), preferred_element_type=jnp.float32)
    unit_text, text_scale = unit_rows(pooled)
    unit_image, image_scale = unit_rows(images.astype(jnp.float32))
    text_half = unit_text.astype(jnp.bfloat16)
    image_half = unit_image.astype(jnp.bfloat16)
    logits = LOGIT_SCALE * lax.dot_general(text_half, image_half, (((1,), (1,)), ((), ())), preferred_element_type=jnp.float32) + LOGIT_SHIFT
    signs = jnp.where(pair_group[:, None] == pair_group[None, :], 1.0, -1.0).astype(jnp.float32)
    caption_loss = -lax.optimization_barrier(jnp.sum(jax.nn.log_sigmoid(signs * logits), 1)) / B_TOTAL
    coef = (-LOGIT_SCALE * signs * jax.nn.sigmoid(-signs * logits)).astype(jnp.bfloat16)
    text_back = jnp.dot(coef, image_half, preferred_element_type=jnp.float32)
    image_back = lax.dot_general(coef, text_half, (((0,), (0,)), ((), ())), preferred_element_type=jnp.float32)
    pooled_grad = (text_back - unit_text * lax.optimization_barrier(jnp.sum(unit_text * text_back, 1, keepdims=True))) * text_scale
    image_grad = (image_back - unit_image * lax.optimization_barrier(jnp.sum(unit_image * image_back, 1, keepdims=True))) * image_scale
    pooled_half = pooled_grad.astype(jnp.bfloat16)
    hidden_grad = jnp.dot(pooled_half, w_down, preferred_element_type=jnp.float32)
    hidden_blocks = hidden_grad.reshape(blocks, B_DEV, FF)

    def backward(total, pieces):
        tok_block, len_block, grad_block = pieces
        normed, value, slope, share, tok_float = front(tok_block, len_block, w_up)
        pre_grad = (share[:, :, None] * grad_block[:, None, :] * slope.reshape(B_DEV, TOKLEN, FF)).astype(jnp.bfloat16)
        pre_grad = pre_grad.reshape(B_DEV * TOKLEN, FF)
        term = lax.dot_general(normed, pre_grad, (((0,), (0,)), ((), ())), preferred_element_type=jnp.float32)
        return (total + term, None)
    up_grad, unused = lax.scan(backward, jnp.zeros((D, FF), jnp.float32), (tok_blocks, len_blocks, hidden_blocks))
    down_grad = lax.dot_general(pooled_half, gbar, (((0,), (0,)), ((), ())), preferred_element_type=jnp.float32)
    return (caption_loss, image_grad, up_grad, down_grad)
```

```python
import jax
import jax.numpy as jnp
from jax import lax
from jax.experimental.layout import Layout, with_layout_constraint
from jax.sharding import PartitionSpec as P

LOGIT_SCALE = 117.0
LOGIT_SHIFT = -12.9


def passed_along(value, axis, steps):
    count = lax.axis_size(axis)
    pairs = [(source, (source + steps) % count) for source in range(count)]
    return lax.ppermute(value, axis, pairs)


def layer_norm(rows):
    center = rows - jnp.mean(rows, -1, keepdims=True)
    spread = jnp.mean(center * center, -1, keepdims=True)
    return center * lax.rsqrt(spread + 1e-06)


def gelu_pair(pre):
    const = 0.7978845608028654
    inner = const * (pre + 0.044715 * pre * pre * pre)
    tanh_u = jnp.tanh(inner)
    value = 0.5 * pre * (1.0 + tanh_u)
    slope = 0.5 * (1.0 + tanh_u) + 0.5 * pre * (1.0 - tanh_u * tanh_u) * const * (
        1.0 + 3.0 * 0.044715 * pre * pre
    )
    return (value, slope)


def unit_rows(rows):
    scale = lax.rsqrt(jnp.sum(rows * rows, 1, keepdims=True) + 1e-06)
    return (rows * scale, scale)


def pair_coef(own_rows, own_group, other_rows, other_group):
    logits = (
        LOGIT_SCALE
        * lax.dot_general(
            own_rows, other_rows, (((1,), (1,)), ((), ())), preferred_element_type=jnp.float32
        )
        + LOGIT_SHIFT
    )
    signs = jnp.where(own_group[:, None] == other_group[None, :], 1.0, -1.0).astype(jnp.float32)
    coef = (-LOGIT_SCALE * signs * jax.nn.sigmoid(-signs * logits)).astype(jnp.bfloat16)
    return (logits, signs, coef)


def on_device(tokens, lengths, images, pair_group, w_up, w_down):
    captions = lengths.shape[0]
    seq_len = tokens.shape[0] // captions
    width = tokens.shape[1]
    hidden = w_up.shape[1]
    devices = lax.axis_size("dp")
    own_index = lax.axis_index("dp")
    total = captions * devices
    own_group = lax.dynamic_slice_in_dim(pair_group, own_index * captions, captions)

    unit_image, image_scale = unit_rows(images.astype(jnp.float32))
    image_half = unit_image.astype(jnp.bfloat16)
    image_all = lax.all_gather(image_half, "dp", tiled=True)

    tok_float = tokens.astype(jnp.float32)
    normed = layer_norm(tok_float).astype(jnp.bfloat16)
    pre = jnp.dot(normed, w_up, preferred_element_type=jnp.float32)
    value, slope = gelu_pair(pre)
    position = jnp.arange(seq_len, dtype=jnp.int32)
    valid = (position[None, :] < lengths[:, None]).astype(jnp.float32)
    share = valid / jnp.sum(valid, 1, keepdims=True)
    gmean = jnp.sum(value.reshape(captions, seq_len, hidden) * share[:, :, None], 1)
    tmean = jnp.sum(tok_float.reshape(captions, seq_len, width) * share[:, :, None], 1)
    gbar = gmean.astype(jnp.bfloat16)
    gbar_all = lax.all_gather(gbar, "dp", tiled=True)
    partial_value = lax.dot_general(
        gbar, w_down, (((1,), (1,)), ((), ())), preferred_element_type=jnp.float32
    )
    pooled = tmean + (partial_value + passed_along(partial_value, "mp", 1))
    unit_text, text_scale = unit_rows(pooled)
    text_half = unit_text.astype(jnp.bfloat16)
    text_all = lax.all_gather(text_half, "dp", tiled=True)

    logits, signs, coef = pair_coef(text_half, own_group, image_all, pair_group)
    caption_loss = -jnp.sum(jax.nn.log_sigmoid(signs * logits), 1) / total
    text_back = jnp.dot(coef, image_all, preferred_element_type=jnp.float32)
    _, _, coef_cols = pair_coef(image_half, own_group, text_all, pair_group)
    img_back = jnp.dot(coef_cols, text_all, preferred_element_type=jnp.float32)

    pooled_grad = (
        text_back - unit_text * jnp.sum(unit_text * text_back, 1, keepdims=True)
    ) * text_scale
    image_grad = (
        img_back - unit_image * jnp.sum(unit_image * img_back, 1, keepdims=True)
    ) * image_scale
    pooled_half = pooled_grad.astype(jnp.bfloat16)
    pooled_all = lax.all_gather(pooled_half, "dp", tiled=True)
    rows = width // devices
    pooled_rows = lax.dynamic_slice_in_dim(pooled_all, own_index * rows, rows, axis=1)
    down_grad = lax.dot_general(
        pooled_rows, gbar_all, (((0,), (0,)), ((), ())), preferred_element_type=jnp.float32
    )
    hidden_grad = jnp.dot(pooled_half, w_down, preferred_element_type=jnp.float32)
    pre_grad = (
        share[:, :, None] * hidden_grad[:, None, :] * slope.reshape(captions, seq_len, hidden)
    ).astype(jnp.bfloat16)
    pre_grad = pre_grad.reshape(captions * seq_len, hidden)
    up_term = lax.dot_general(
        normed.reshape(captions * seq_len, devices, rows),
        pre_grad,
        (((0,), (0,)), ((), ())),
        preferred_element_type=jnp.float32,
    )
    up_term = with_layout_constraint(up_term, Layout(major_to_minor=(0, 1, 2)))
    up_grad = lax.psum_scatter(up_term, "dp", scatter_dimension=0, tiled=False)
    return (caption_loss, image_grad, up_grad, down_grad)


def solution(mesh):
    in_specs = (P("dp", None), P("dp"), P("dp", None), P(), P(None, "mp"), P(None, "mp"))
    out_specs = (P("dp"), P("dp", None), P("dp", "mp"), P("dp", "mp"))
    return jax.shard_map(
        on_device, mesh=mesh, in_specs=in_specs, out_specs=out_specs, check_vma=False
    )
```

```python
import jax
import jax.numpy as jnp
from jax import lax
from jax.sharding import PartitionSpec as P

LOGIT_SCALE = 117.0
LOGIT_SHIFT = -12.9
RS_ORDER = (0, 3, 1, 4, 2, 5)


def passed_along(value, axis, steps):
    count = lax.axis_size(axis)
    pairs = [(source, (source + steps) % count) for source in range(count)]
    return lax.ppermute(value, axis, pairs)


def layer_norm(rows):
    center = rows - jnp.mean(rows, -1, keepdims=True)
    spread = jnp.mean(center * center, -1, keepdims=True)
    return center * lax.rsqrt(spread + 1e-06)


def gelu_pair(pre):
    const = 0.7978845608028654
    inner = const * (pre + 0.044715 * pre * pre * pre)
    tanh_u = jnp.tanh(inner)
    value = 0.5 * pre * (1.0 + tanh_u)
    slope = 0.5 * (1.0 + tanh_u) + 0.5 * pre * (1.0 - tanh_u * tanh_u) * const * (
        1.0 + 3.0 * 0.044715 * pre * pre
    )
    return (value, slope)


def unit_rows(rows):
    scale = lax.rsqrt(jnp.sum(rows * rows, 1, keepdims=True) + 1e-06)
    return (rows * scale, scale)


def pair_coef(own_rows, own_group, other_rows, other_group):
    logits = (
        LOGIT_SCALE
        * lax.dot_general(
            own_rows, other_rows, (((1,), (1,)), ((), ())), preferred_element_type=jnp.float32
        )
        + LOGIT_SHIFT
    )
    signs = jnp.where(own_group[:, None] == other_group[None, :], 1.0, -1.0).astype(jnp.float32)
    coef = (-LOGIT_SCALE * signs * jax.nn.sigmoid(-signs * logits)).astype(jnp.bfloat16)
    return (logits, signs, coef)


def reduce_scatter_halving(blocks, axis, order):
    devices = lax.axis_size(axis)
    own_index = lax.axis_index(axis)
    depth = devices.bit_length() - 1
    left = list(range(depth - 1, -1, -1))
    state = blocks.reshape((2,) * depth + blocks.shape[1:])
    for bit in order:
        place = left.index(bit)
        own_bit = (own_index >> bit) & 1
        keep = lax.dynamic_index_in_dim(state, own_bit, axis=place, keepdims=False)
        send = lax.dynamic_index_in_dim(state, 1 - own_bit, axis=place, keepdims=False)
        pairs = [(source, source ^ (1 << bit)) for source in range(devices)]
        state = keep + lax.ppermute(send, axis, pairs)
        left.remove(bit)
    return state


def on_device(tokens, lengths, images, pair_group, w_up, w_down):
    captions = lengths.shape[0]
    seq_len = tokens.shape[0] // captions
    width = tokens.shape[1]
    hidden = w_up.shape[1]
    devices = lax.axis_size("dp")
    own_index = lax.axis_index("dp")
    total = captions * devices
    rows = width // devices
    own_group = lax.dynamic_slice_in_dim(pair_group, own_index * captions, captions)

    unit_image, image_scale = unit_rows(images.astype(jnp.float32))
    image_half = unit_image.astype(jnp.bfloat16)
    image_all = lax.all_gather(image_half, "dp", tiled=True)

    tok_float = tokens.astype(jnp.float32)
    normed = layer_norm(tok_float).astype(jnp.bfloat16)
    pre = jnp.dot(normed, w_up, preferred_element_type=jnp.float32)
    value, slope = gelu_pair(pre)
    position = jnp.arange(seq_len, dtype=jnp.int32)
    valid = (position[None, :] < lengths[:, None]).astype(jnp.float32)
    share = valid / jnp.sum(valid, 1, keepdims=True)
    gmean = jnp.sum(value.reshape(captions, seq_len, hidden) * share[:, :, None], 1)
    tmean = jnp.sum(tok_float.reshape(captions, seq_len, width) * share[:, :, None], 1)
    gbar = gmean.astype(jnp.bfloat16)
    partial_value = lax.dot_general(
        gbar, w_down, (((1,), (1,)), ((), ())), preferred_element_type=jnp.float32
    )
    pooled = tmean + (partial_value + passed_along(partial_value, "mp", 1))
    gathered = lax.all_gather(
        jnp.concatenate([pooled, gbar.astype(jnp.float32)], 1), "dp", tiled=True
    )
    pooled_all = gathered[:, :width]
    gbar_all = gathered[:, width:].astype(jnp.bfloat16)

    unit_text, text_scale = unit_rows(pooled_all)
    text_all = unit_text.astype(jnp.bfloat16)
    logits, signs, coef = pair_coef(text_all, pair_group, image_all, pair_group)
    own_logits = lax.dynamic_slice_in_dim(logits, own_index * captions, captions)
    own_signs = lax.dynamic_slice_in_dim(signs, own_index * captions, captions)
    caption_loss = -jnp.sum(jax.nn.log_sigmoid(own_signs * own_logits), 1) / total
    text_back = jnp.dot(coef, image_all, preferred_element_type=jnp.float32)
    coef_cols = lax.dynamic_slice_in_dim(coef, own_index * captions, captions, axis=1)
    img_back = lax.dot_general(
        coef_cols, text_all, (((0,), (0,)), ((), ())), preferred_element_type=jnp.float32
    )

    pooled_grad = (
        text_back - unit_text * jnp.sum(unit_text * text_back, 1, keepdims=True)
    ) * text_scale
    image_grad = (
        img_back - unit_image * jnp.sum(unit_image * img_back, 1, keepdims=True)
    ) * image_scale
    pooled_all_half = pooled_grad.astype(jnp.bfloat16)
    pooled_half = lax.dynamic_slice_in_dim(pooled_all_half, own_index * captions, captions)
    pooled_rows = lax.dynamic_slice_in_dim(pooled_all_half, own_index * rows, rows, axis=1)
    down_grad = lax.dot_general(
        pooled_rows, gbar_all, (((0,), (0,)), ((), ())), preferred_element_type=jnp.float32
    )
    hidden_grad = jnp.dot(pooled_half, w_down, preferred_element_type=jnp.float32)
    pre_grad = (
        share[:, :, None] * hidden_grad[:, None, :] * slope.reshape(captions, seq_len, hidden)
    ).astype(jnp.bfloat16)
    pre_grad = pre_grad.reshape(captions * seq_len, hidden)
    up_term = lax.dot_general(
        normed.reshape(captions * seq_len, devices, rows),
        pre_grad,
        (((0,), (0,)), ((), ())),
        preferred_element_type=jnp.float32,
    )
    up_grad = reduce_scatter_halving(up_term, "dp", RS_ORDER)
    return (caption_loss, image_grad, up_grad, down_grad)


def solution(mesh):
    in_specs = (P("dp", None), P("dp"), P("dp", None), P(), P(None, "mp"), P(None, "mp"))
    out_specs = (P("dp"), P("dp", None), P("dp", "mp"), P("dp", "mp"))
    return jax.shard_map(
        on_device, mesh=mesh, in_specs=in_specs, out_specs=out_specs, check_vma=False
    )
```

```python
import jax
import jax.numpy as jnp
from jax import lax
from jax.sharding import PartitionSpec as P

LOGIT_SCALE = 117.0
LOGIT_SHIFT = -12.9
RS_ORDER = (0, 3, 1, 4, 2, 5)


def passed_along(value, axis, steps):
    count = lax.axis_size(axis)
    pairs = [(source, (source + steps) % count) for source in range(count)]
    return lax.ppermute(value, axis, pairs)


def layer_norm(rows):
    center = rows - jnp.mean(rows, -1, keepdims=True)
    spread = jnp.mean(center * center, -1, keepdims=True)
    return center * lax.rsqrt(spread + 1e-06)


def gelu_pair(pre):
    const = 0.7978845608028654
    inner = const * (pre + 0.044715 * pre * pre * pre)
    tanh_u = jnp.tanh(inner)
    value = 0.5 * pre * (1.0 + tanh_u)
    slope = 0.5 * (1.0 + tanh_u) + 0.5 * pre * (1.0 - tanh_u * tanh_u) * const * (
        1.0 + 3.0 * 0.044715 * pre * pre
    )
    return (value, slope)


def unit_rows(rows):
    scale = lax.rsqrt(jnp.sum(rows * rows, 1, keepdims=True) + 1e-06)
    return (rows * scale, scale)


def pair_coef(own_rows, own_group, other_rows, other_group):
    logits = (
        LOGIT_SCALE
        * lax.dot_general(
            own_rows, other_rows, (((1,), (1,)), ((), ())), preferred_element_type=jnp.float32
        )
        + LOGIT_SHIFT
    )
    signs = jnp.where(own_group[:, None] == other_group[None, :], 1.0, -1.0).astype(jnp.float32)
    coef = (-LOGIT_SCALE * signs * jax.nn.sigmoid(-signs * logits)).astype(jnp.bfloat16)
    return (logits, signs, coef)


def reduce_scatter_halving(blocks, axis, order):
    devices = lax.axis_size(axis)
    own_index = lax.axis_index(axis)
    depth = devices.bit_length() - 1
    left = list(range(depth - 1, -1, -1))
    state = blocks.reshape((2,) * depth + blocks.shape[1:])
    for bit in order:
        place = left.index(bit)
        own_bit = (own_index >> bit) & 1
        keep = lax.dynamic_index_in_dim(state, own_bit, axis=place, keepdims=False)
        send = lax.dynamic_index_in_dim(state, 1 - own_bit, axis=place, keepdims=False)
        pairs = [(source, source ^ (1 << bit)) for source in range(devices)]
        state = keep + lax.ppermute(send, axis, pairs)
        left.remove(bit)
    return state


def all_gather_doubling(block, axis, order):
    devices = lax.axis_size(axis)
    own_index = lax.axis_index(axis)
    depth = devices.bit_length() - 1
    state = block[None]
    gathered = []
    for bit in order:
        place = sum(1 for done in gathered if done > bit)
        pairs = [(source, source ^ (1 << bit)) for source in range(devices)]
        other = lax.ppermute(state, axis, pairs)
        low_first = jnp.stack([state, other], axis=place)
        high_first = jnp.stack([other, state], axis=place)
        state = jnp.where(((own_index >> bit) & 1) == 0, low_first, high_first)
        gathered.append(bit)
    return state.reshape((devices * block.shape[0],) + block.shape[1:])


def on_device(tokens, lengths, images, pair_group, w_up, w_down):
    captions = lengths.shape[0]
    seq_len = tokens.shape[0] // captions
    width = tokens.shape[1]
    hidden = w_up.shape[1]
    devices = lax.axis_size("dp")
    own_index = lax.axis_index("dp")
    total = captions * devices
    rows = width // devices
    own_group = lax.dynamic_slice_in_dim(pair_group, own_index * captions, captions)

    unit_image, image_scale = unit_rows(images.astype(jnp.float32))
    image_half = unit_image.astype(jnp.bfloat16)
    image_all = all_gather_doubling(image_half, "dp", RS_ORDER[::-1])

    tok_float = tokens.astype(jnp.float32)
    normed = layer_norm(tok_float).astype(jnp.bfloat16)
    pre = jnp.dot(normed, w_up, preferred_element_type=jnp.float32)
    value, slope = gelu_pair(pre)
    position = jnp.arange(seq_len, dtype=jnp.int32)
    valid = (position[None, :] < lengths[:, None]).astype(jnp.float32)
    share = valid / jnp.sum(valid, 1, keepdims=True)
    gmean = jnp.sum(value.reshape(captions, seq_len, hidden) * share[:, :, None], 1)
    tmean = jnp.sum(tok_float.reshape(captions, seq_len, width) * share[:, :, None], 1)
    gbar = gmean.astype(jnp.bfloat16)
    partial_value = lax.dot_general(
        gbar, w_down, (((1,), (1,)), ((), ())), preferred_element_type=jnp.float32
    )
    pooled = tmean + (partial_value + passed_along(partial_value, "mp", 1))
    gathered = lax.all_gather(
        jnp.concatenate([pooled, gbar.astype(jnp.float32)], 1), "dp", tiled=True
    )
    pooled_all = gathered[:, :width]
    gbar_all = gathered[:, width:].astype(jnp.bfloat16)

    unit_text, text_scale = unit_rows(pooled_all)
    text_all = unit_text.astype(jnp.bfloat16)
    logits, signs, coef = pair_coef(text_all, pair_group, image_all, pair_group)
    own_logits = lax.dynamic_slice_in_dim(logits, own_index * captions, captions)
    own_signs = lax.dynamic_slice_in_dim(signs, own_index * captions, captions)
    caption_loss = -jnp.sum(jax.nn.log_sigmoid(own_signs * own_logits), 1) / total
    text_back = jnp.dot(coef, image_all, preferred_element_type=jnp.float32)
    coef_cols = lax.dynamic_slice_in_dim(coef, own_index * captions, captions, axis=1)
    img_back = lax.dot_general(
        coef_cols, text_all, (((0,), (0,)), ((), ())), preferred_element_type=jnp.float32
    )

    pooled_grad = (
        text_back - unit_text * jnp.sum(unit_text * text_back, 1, keepdims=True)
    ) * text_scale
    image_grad = (
        img_back - unit_image * jnp.sum(unit_image * img_back, 1, keepdims=True)
    ) * image_scale
    pooled_all_half = pooled_grad.astype(jnp.bfloat16)
    pooled_half = lax.dynamic_slice_in_dim(pooled_all_half, own_index * captions, captions)
    pooled_rows = lax.dynamic_slice_in_dim(pooled_all_half, own_index * rows, rows, axis=1)
    down_grad = lax.dot_general(
        pooled_rows, gbar_all, (((0,), (0,)), ((), ())), preferred_element_type=jnp.float32
    )
    hidden_grad = jnp.dot(pooled_half, w_down, preferred_element_type=jnp.float32)
    pre_grad = (
        share[:, :, None] * hidden_grad[:, None, :] * slope.reshape(captions, seq_len, hidden)
    ).astype(jnp.bfloat16)
    pre_grad = pre_grad.reshape(captions * seq_len, hidden)
    up_term = lax.dot_general(
        normed.reshape(captions * seq_len, devices, rows),
        pre_grad,
        (((0,), (0,)), ((), ())),
        preferred_element_type=jnp.float32,
    )
    up_grad = reduce_scatter_halving(up_term, "dp", RS_ORDER)
    return (caption_loss, image_grad, up_grad, down_grad)


def solution(mesh):
    in_specs = (P("dp", None), P("dp"), P("dp", None), P(), P(None, "mp"), P(None, "mp"))
    out_specs = (P("dp"), P("dp", None), P("dp", "mp"), P("dp", "mp"))
    return jax.shard_map(
        on_device, mesh=mesh, in_specs=in_specs, out_specs=out_specs, check_vma=False
    )
```

```python
import jax
import jax.numpy as jnp
from jax import lax
from jax.sharding import PartitionSpec as P

LOGIT_SCALE = 117.0
LOGIT_SHIFT = -12.9
RS_ORDER = (0, 3, 1, 4, 2, 5)


def passed_along(value, axis, steps):
    count = lax.axis_size(axis)
    pairs = [(source, (source + steps) % count) for source in range(count)]
    return lax.ppermute(value, axis, pairs)


def layer_norm(rows):
    center = rows - jnp.mean(rows, -1, keepdims=True)
    spread = jnp.mean(center * center, -1, keepdims=True)
    return center * lax.rsqrt(spread + 1e-06)


def gelu_pair(pre):
    const = 0.7978845608028654
    inner = const * (pre + 0.044715 * pre * pre * pre)
    tanh_u = jnp.tanh(inner)
    value = 0.5 * pre * (1.0 + tanh_u)
    slope = 0.5 * (1.0 + tanh_u) + 0.5 * pre * (1.0 - tanh_u * tanh_u) * const * (
        1.0 + 3.0 * 0.044715 * pre * pre
    )
    return (value, slope)


def unit_rows(rows):
    scale = lax.rsqrt(jnp.sum(rows * rows, 1, keepdims=True) + 1e-06)
    return (rows * scale, scale)


def pair_coef(own_rows, own_group, other_rows, other_group):
    logits = (
        LOGIT_SCALE
        * lax.dot_general(
            own_rows, other_rows, (((1,), (1,)), ((), ())), preferred_element_type=jnp.float32
        )
        + LOGIT_SHIFT
    )
    signs = jnp.where(own_group[:, None] == other_group[None, :], 1.0, -1.0).astype(jnp.float32)
    coef = (-LOGIT_SCALE * signs * jax.nn.sigmoid(-signs * logits)).astype(jnp.bfloat16)
    return (logits, signs, coef)


def reduce_scatter_halving(blocks, axis, order):
    devices = lax.axis_size(axis)
    own_index = lax.axis_index(axis)
    depth = devices.bit_length() - 1
    left = list(range(depth - 1, -1, -1))
    state = blocks.reshape((2,) * depth + blocks.shape[1:])
    for bit in order:
        place = left.index(bit)
        own_bit = (own_index >> bit) & 1
        keep = lax.dynamic_index_in_dim(state, own_bit, axis=place, keepdims=False)
        send = lax.dynamic_index_in_dim(state, 1 - own_bit, axis=place, keepdims=False)
        pairs = [(source, source ^ (1 << bit)) for source in range(devices)]
        state = keep + lax.ppermute(send, axis, pairs)
        left.remove(bit)
    return state


def all_gather_doubling(block, axis, order):
    devices = lax.axis_size(axis)
    own_index = lax.axis_index(axis)
    depth = devices.bit_length() - 1
    state = block[None]
    gathered = []
    for bit in order:
        place = sum(1 for done in gathered if done > bit)
        pairs = [(source, source ^ (1 << bit)) for source in range(devices)]
        other = lax.ppermute(state, axis, pairs)
        low_first = jnp.stack([state, other], axis=place)
        high_first = jnp.stack([other, state], axis=place)
        state = jnp.where(((own_index >> bit) & 1) == 0, low_first, high_first)
        gathered.append(bit)
    return state.reshape((devices * block.shape[0],) + block.shape[1:])


def on_device(tokens, lengths, images, pair_group, w_up, w_down):
    captions = lengths.shape[0]
    seq_len = tokens.shape[0] // captions
    width = tokens.shape[1]
    hidden = w_up.shape[1]
    devices = lax.axis_size("dp")
    own_index = lax.axis_index("dp")
    total = captions * devices
    rows = width // devices
    own_group = lax.dynamic_slice_in_dim(pair_group, own_index * captions, captions)

    unit_image, image_scale = unit_rows(images.astype(jnp.float32))
    image_half = unit_image.astype(jnp.bfloat16)

    tok_float = tokens.astype(jnp.float32)
    normed = layer_norm(tok_float).astype(jnp.bfloat16)
    pre = jnp.dot(normed, w_up, preferred_element_type=jnp.float32)
    value, slope = gelu_pair(pre)
    position = jnp.arange(seq_len, dtype=jnp.int32)
    valid = (position[None, :] < lengths[:, None]).astype(jnp.float32)
    share = valid / jnp.sum(valid, 1, keepdims=True)
    gmean = jnp.sum(value.reshape(captions, seq_len, hidden) * share[:, :, None], 1)
    tmean = jnp.sum(tok_float.reshape(captions, seq_len, width) * share[:, :, None], 1)
    gbar = gmean.astype(jnp.bfloat16)
    gbar_all = lax.all_gather(gbar, "dp", tiled=True)
    partial_value = lax.dot_general(
        gbar, w_down, (((1,), (1,)), ((), ())), preferred_element_type=jnp.float32
    )
    pooled = tmean + (partial_value + passed_along(partial_value, "mp", 1))
    unit_text, text_scale = unit_rows(pooled)
    text_half = unit_text.astype(jnp.bfloat16)
    both_all = all_gather_doubling(
        jnp.concatenate([text_half, image_half], 1), "dp", RS_ORDER[::-1]
    )
    text_all = both_all[:, :width]
    image_all = both_all[:, width:]

    logits, signs, coef = pair_coef(text_half, own_group, image_all, pair_group)
    caption_loss = -jnp.sum(jax.nn.log_sigmoid(signs * logits), 1) / total
    text_back = jnp.dot(coef, image_all, preferred_element_type=jnp.float32)
    _, _, coef_cols = pair_coef(image_half, own_group, text_all, pair_group)
    img_back = jnp.dot(coef_cols, text_all, preferred_element_type=jnp.float32)

    pooled_grad = (
        text_back - unit_text * jnp.sum(unit_text * text_back, 1, keepdims=True)
    ) * text_scale
    image_grad = (
        img_back - unit_image * jnp.sum(unit_image * img_back, 1, keepdims=True)
    ) * image_scale
    pooled_half = pooled_grad.astype(jnp.bfloat16)
    pooled_all = lax.all_gather(pooled_half, "dp", tiled=True)
    pooled_rows = lax.dynamic_slice_in_dim(pooled_all, own_index * rows, rows, axis=1)
    down_grad = lax.dot_general(
        pooled_rows, gbar_all, (((0,), (0,)), ((), ())), preferred_element_type=jnp.float32
    )
    hidden_grad = jnp.dot(pooled_half, w_down, preferred_element_type=jnp.float32)
    pre_grad = (
        share[:, :, None] * hidden_grad[:, None, :] * slope.reshape(captions, seq_len, hidden)
    ).astype(jnp.bfloat16)
    pre_grad = pre_grad.reshape(captions * seq_len, hidden)
    up_term = lax.dot_general(
        normed.reshape(captions * seq_len, devices, rows),
        pre_grad,
        (((0,), (0,)), ((), ())),
        preferred_element_type=jnp.float32,
    )
    up_grad = reduce_scatter_halving(up_term, "dp", RS_ORDER)
    return (caption_loss, image_grad, up_grad, down_grad)


def solution(mesh):
    in_specs = (P("dp", None), P("dp"), P("dp", None), P(), P(None, "mp"), P(None, "mp"))
    out_specs = (P("dp"), P("dp", None), P("dp", "mp"), P("dp", "mp"))
    return jax.shard_map(
        on_device, mesh=mesh, in_specs=in_specs, out_specs=out_specs, check_vma=False
    )
```

```python
import jax
import jax.numpy as jnp
from jax import lax
from jax.sharding import PartitionSpec as P

LOGIT_SCALE = 117.0
LOGIT_SHIFT = -12.9
RS_ORDER = (0, 3, 1, 4, 2, 5)


def passed_along(value, axis, steps):
    count = lax.axis_size(axis)
    pairs = [(source, (source + steps) % count) for source in range(count)]
    return lax.ppermute(value, axis, pairs)


def layer_norm(rows):
    center = rows - jnp.mean(rows, -1, keepdims=True)
    spread = jnp.mean(center * center, -1, keepdims=True)
    return center * lax.rsqrt(spread + 1e-06)


def gelu_pair(pre):
    const = 0.7978845608028654
    inner = const * (pre + 0.044715 * pre * pre * pre)
    tanh_u = jnp.tanh(inner)
    value = 0.5 * pre * (1.0 + tanh_u)
    slope = 0.5 * (1.0 + tanh_u) + 0.5 * pre * (1.0 - tanh_u * tanh_u) * const * (
        1.0 + 3.0 * 0.044715 * pre * pre
    )
    return (value, slope)


def unit_rows(rows):
    scale = lax.rsqrt(jnp.sum(rows * rows, 1, keepdims=True) + 1e-06)
    return (rows * scale, scale)


def pair_coef(own_rows, own_group, other_rows, other_group):
    logits = (
        LOGIT_SCALE
        * lax.dot_general(
            own_rows, other_rows, (((1,), (1,)), ((), ())), preferred_element_type=jnp.float32
        )
        + LOGIT_SHIFT
    )
    signs = jnp.where(own_group[:, None] == other_group[None, :], 1.0, -1.0).astype(jnp.float32)
    coef = (-LOGIT_SCALE * signs * jax.nn.sigmoid(-signs * logits)).astype(jnp.bfloat16)
    return (logits, signs, coef)


def reduce_scatter_halving(blocks, axis, order):
    devices = lax.axis_size(axis)
    own_index = lax.axis_index(axis)
    depth = devices.bit_length() - 1
    left = list(range(depth - 1, -1, -1))
    state = blocks.reshape((2,) * depth + blocks.shape[1:])
    for bit in order:
        place = left.index(bit)
        own_bit = (own_index >> bit) & 1
        keep = lax.dynamic_index_in_dim(state, own_bit, axis=place, keepdims=False)
        send = lax.dynamic_index_in_dim(state, 1 - own_bit, axis=place, keepdims=False)
        pairs = [(source, source ^ (1 << bit)) for source in range(devices)]
        state = keep + lax.ppermute(send, axis, pairs)
        left.remove(bit)
    return state


def all_gather_doubling(block, axis, order):
    devices = lax.axis_size(axis)
    own_index = lax.axis_index(axis)
    depth = devices.bit_length() - 1
    state = block[None]
    gathered = []
    for bit in order:
        place = sum(1 for done in gathered if done > bit)
        pairs = [(source, source ^ (1 << bit)) for source in range(devices)]
        other = lax.ppermute(state, axis, pairs)
        low_first = jnp.stack([state, other], axis=place)
        high_first = jnp.stack([other, state], axis=place)
        state = jnp.where(((own_index >> bit) & 1) == 0, low_first, high_first)
        gathered.append(bit)
    return state.reshape((devices * block.shape[0],) + block.shape[1:])


def on_device(tokens, lengths, images, pair_group, w_up, w_down):
    captions = lengths.shape[0]
    seq_len = tokens.shape[0] // captions
    width = tokens.shape[1]
    hidden = w_up.shape[1]
    devices = lax.axis_size("dp")
    own_index = lax.axis_index("dp")
    total = captions * devices
    rows = width // devices
    own_group = lax.dynamic_slice_in_dim(pair_group, own_index * captions, captions)

    unit_image, image_scale = unit_rows(images.astype(jnp.float32))
    image_half = unit_image.astype(jnp.bfloat16)

    tok_float = tokens.astype(jnp.float32)
    normed = layer_norm(tok_float).astype(jnp.bfloat16)
    pre = jnp.dot(normed, w_up, preferred_element_type=jnp.float32)
    value, slope = gelu_pair(pre)
    position = jnp.arange(seq_len, dtype=jnp.int32)
    valid = (position[None, :] < lengths[:, None]).astype(jnp.float32)
    share = valid / jnp.sum(valid, 1, keepdims=True)
    gmean = jnp.sum(value.reshape(captions, seq_len, hidden) * share[:, :, None], 1)
    tmean = jnp.sum(tok_float.reshape(captions, seq_len, width) * share[:, :, None], 1)
    gbar = gmean.astype(jnp.bfloat16)
    gbar_all = lax.all_gather(gbar, "dp", tiled=True)
    partial_value = lax.dot_general(
        gbar, w_down, (((1,), (1,)), ((), ())), preferred_element_type=jnp.float32
    )
    pooled = tmean + (partial_value + passed_along(partial_value, "mp", 1))
    unit_text, text_scale = unit_rows(pooled)
    text_half = unit_text.astype(jnp.bfloat16)
    both_all = all_gather_doubling(
        jnp.concatenate([text_half, image_half], 1), "dp", RS_ORDER[::-1]
    )
    text_all = both_all[:, :width]
    image_all = both_all[:, width:]

    logits, signs, coef = pair_coef(text_half, own_group, image_all, pair_group)
    caption_loss = -jnp.sum(jax.nn.log_sigmoid(signs * logits), 1) / total
    text_back = jnp.dot(coef, image_all, preferred_element_type=jnp.float32)
    _, _, coef_cols = pair_coef(image_half, own_group, text_all, pair_group)
    img_back = jnp.dot(coef_cols, text_all, preferred_element_type=jnp.float32)

    pooled_grad = (
        text_back - unit_text * jnp.sum(unit_text * text_back, 1, keepdims=True)
    ) * text_scale
    image_grad = (
        img_back - unit_image * jnp.sum(unit_image * img_back, 1, keepdims=True)
    ) * image_scale
    pooled_half = pooled_grad.astype(jnp.bfloat16)
    pooled_rows = lax.all_to_all(
        pooled_half.reshape(captions, devices, rows), "dp", 1, 0
    ).reshape(total, rows)
    down_grad = lax.dot_general(
        pooled_rows, gbar_all, (((0,), (0,)), ((), ())), preferred_element_type=jnp.float32
    )
    hidden_grad = jnp.dot(pooled_half, w_down, preferred_element_type=jnp.float32)
    pre_grad = (
        share[:, :, None] * hidden_grad[:, None, :] * slope.reshape(captions, seq_len, hidden)
    ).astype(jnp.bfloat16)
    pre_grad = pre_grad.reshape(captions * seq_len, hidden)
    up_term = lax.dot_general(
        normed.reshape(captions * seq_len, devices, rows),
        pre_grad,
        (((0,), (0,)), ((), ())),
        preferred_element_type=jnp.float32,
    )
    up_grad = reduce_scatter_halving(up_term, "dp", RS_ORDER)
    return (caption_loss, image_grad, up_grad, down_grad)


def solution(mesh):
    in_specs = (P("dp", None), P("dp"), P("dp", None), P(), P(None, "mp"), P(None, "mp"))
    out_specs = (P("dp"), P("dp", None), P("dp", "mp"), P("dp", "mp"))
    return jax.shard_map(
        on_device, mesh=mesh, in_specs=in_specs, out_specs=out_specs, check_vma=False
    )
```

```python
import jax
import jax.numpy as jnp
from jax import lax
from jax.sharding import PartitionSpec as P

LOGIT_SCALE = 117.0
LOGIT_SHIFT = -12.9
RS_ORDER = (0, 3, 1, 4, 2, 5)
RS_TWIN = (0, 4, 3, 1, 5, 2)


def passed_along(value, axis, steps):
    count = lax.axis_size(axis)
    pairs = [(source, (source + steps) % count) for source in range(count)]
    return lax.ppermute(value, axis, pairs)


def layer_norm(rows):
    center = rows - jnp.mean(rows, -1, keepdims=True)
    spread = jnp.mean(center * center, -1, keepdims=True)
    return center * lax.rsqrt(spread + 1e-06)


def gelu_pair(pre):
    const = 0.7978845608028654
    inner = const * (pre + 0.044715 * pre * pre * pre)
    tanh_u = jnp.tanh(inner)
    value = 0.5 * pre * (1.0 + tanh_u)
    slope = 0.5 * (1.0 + tanh_u) + 0.5 * pre * (1.0 - tanh_u * tanh_u) * const * (
        1.0 + 3.0 * 0.044715 * pre * pre
    )
    return (value, slope)


def unit_rows(rows):
    scale = lax.rsqrt(jnp.sum(rows * rows, 1, keepdims=True) + 1e-06)
    return (rows * scale, scale)


def pair_coef(own_rows, own_group, other_rows, other_group):
    logits = (
        LOGIT_SCALE
        * lax.dot_general(
            own_rows, other_rows, (((1,), (1,)), ((), ())), preferred_element_type=jnp.float32
        )
        + LOGIT_SHIFT
    )
    signs = jnp.where(own_group[:, None] == other_group[None, :], 1.0, -1.0).astype(jnp.float32)
    coef = (-LOGIT_SCALE * signs * jax.nn.sigmoid(-signs * logits)).astype(jnp.bfloat16)
    return (logits, signs, coef)


def permuted_blocks(blocks, depth, first, second):
    lead = blocks.shape[:1]
    swap = dict(zip(first, second))
    split = blocks.reshape(lead + (2,) * depth + blocks.shape[2:])
    moved = [1 + depth - 1 - swap[depth - 1 - place] for place in range(depth)]
    axes = [0] + moved + list(range(1 + depth, split.ndim))
    return jnp.transpose(split, axes).reshape(blocks.shape)


def first_stage_halves(natural, permuted, variant):
    shape = natural.shape
    halves = shape[:1] + (shape[1] // 2, 2) + shape[2:]
    own = jnp.where(variant == 0, natural, permuted).reshape(halves)
    other = jnp.where(variant == 0, permuted, natural).reshape(halves)
    keep = lax.dynamic_index_in_dim(own, variant, axis=2, keepdims=False)
    send = lax.dynamic_index_in_dim(other, 1 - variant, axis=2, keepdims=False)
    return (keep, send)


def reduce_scatter_halving(keep, send, axis, first, second):
    devices = lax.axis_size(axis)
    own_index = lax.axis_index(axis)
    depth = devices.bit_length() - 1
    pairs = [(source, source ^ 1) for source in range(devices)]
    state = keep + lax.ppermute(send, axis, pairs)
    left = list(range(depth - 1, 0, -1))
    state = state.reshape((2,) * (depth - 1) + state.shape[1:])
    variant = own_index & 1
    for bit, twin in zip(first[1:], second[1:]):
        place = left.index(bit)
        own_bit = jnp.where(variant == 0, (own_index >> bit) & 1, (own_index >> twin) & 1)
        keep = lax.dynamic_index_in_dim(state, own_bit, axis=place, keepdims=False)
        send = lax.dynamic_index_in_dim(state, 1 - own_bit, axis=place, keepdims=False)
        pairs = [
            (source, source ^ (1 << (bit if source & 1 == 0 else twin)))
            for source in range(devices)
        ]
        state = keep + lax.ppermute(send, axis, pairs)
        left.remove(bit)
    return state


def all_gather_doubling(block, axis, order):
    devices = lax.axis_size(axis)
    own_index = lax.axis_index(axis)
    depth = devices.bit_length() - 1
    state = block[None]
    gathered = []
    for bit in order:
        place = sum(1 for done in gathered if done > bit)
        pairs = [(source, source ^ (1 << bit)) for source in range(devices)]
        other = lax.ppermute(state, axis, pairs)
        low_first = jnp.stack([state, other], axis=place)
        high_first = jnp.stack([other, state], axis=place)
        state = jnp.where(((own_index >> bit) & 1) == 0, low_first, high_first)
        gathered.append(bit)
    return state.reshape((devices * block.shape[0],) + block.shape[1:])


def on_device(tokens, lengths, images, pair_group, w_up, w_down):
    captions = lengths.shape[0]
    seq_len = tokens.shape[0] // captions
    width = tokens.shape[1]
    hidden = w_up.shape[1]
    devices = lax.axis_size("dp")
    own_index = lax.axis_index("dp")
    total = captions * devices
    rows = width // devices
    own_group = lax.dynamic_slice_in_dim(pair_group, own_index * captions, captions)

    unit_image, image_scale = unit_rows(images.astype(jnp.float32))
    image_half = unit_image.astype(jnp.bfloat16)

    tok_float = tokens.astype(jnp.float32)
    normed = layer_norm(tok_float).astype(jnp.bfloat16)
    pre = jnp.dot(normed, w_up, preferred_element_type=jnp.float32)
    value, slope = gelu_pair(pre)
    position = jnp.arange(seq_len, dtype=jnp.int32)
    valid = (position[None, :] < lengths[:, None]).astype(jnp.float32)
    share = valid / jnp.sum(valid, 1, keepdims=True)
    gmean = jnp.sum(value.reshape(captions, seq_len, hidden) * share[:, :, None], 1)
    tmean = jnp.sum(tok_float.reshape(captions, seq_len, width) * share[:, :, None], 1)
    gbar = gmean.astype(jnp.bfloat16)
    gbar_all = lax.all_gather(gbar, "dp", tiled=True)
    partial_value = lax.dot_general(
        gbar, w_down, (((1,), (1,)), ((), ())), preferred_element_type=jnp.float32
    )
    pooled = tmean + (partial_value + passed_along(partial_value, "mp", 1))
    unit_text, text_scale = unit_rows(pooled)
    text_half = unit_text.astype(jnp.bfloat16)
    both_all = all_gather_doubling(
        jnp.concatenate([text_half, image_half], 1), "dp", RS_ORDER[::-1]
    )
    text_all = both_all[:, :width]
    image_all = both_all[:, width:]

    logits, signs, coef = pair_coef(text_half, own_group, image_all, pair_group)
    caption_loss = -jnp.sum(jax.nn.log_sigmoid(signs * logits), 1) / total
    text_back = jnp.dot(coef, image_all, preferred_element_type=jnp.float32)
    _, _, coef_cols = pair_coef(image_half, own_group, text_all, pair_group)
    img_back = jnp.dot(coef_cols, text_all, preferred_element_type=jnp.float32)

    pooled_grad = (
        text_back - unit_text * jnp.sum(unit_text * text_back, 1, keepdims=True)
    ) * text_scale
    image_grad = (
        img_back - unit_image * jnp.sum(unit_image * img_back, 1, keepdims=True)
    ) * image_scale
    pooled_half = pooled_grad.astype(jnp.bfloat16)
    pooled_rows = lax.all_to_all(
        pooled_half.reshape(captions, devices, rows), "dp", 1, 0
    ).reshape(total, rows)
    down_grad = lax.dot_general(
        pooled_rows, gbar_all, (((0,), (0,)), ((), ())), preferred_element_type=jnp.float32
    )
    hidden_grad = jnp.dot(pooled_half, w_down, preferred_element_type=jnp.float32)
    pre_grad = (
        share[:, :, None] * hidden_grad[:, None, :] * slope.reshape(captions, seq_len, hidden)
    ).astype(jnp.bfloat16)
    pre_grad = pre_grad.reshape(captions * seq_len, hidden)
    normed_blocks = normed.reshape(captions * seq_len, devices, rows)
    depth = devices.bit_length() - 1
    keep_rows, send_rows = first_stage_halves(
        normed_blocks,
        permuted_blocks(normed_blocks, depth, RS_ORDER, RS_TWIN),
        own_index & 1,
    )
    keep_term, send_term = [
        lax.dot_general(
            part, pre_grad, (((0,), (0,)), ((), ())), preferred_element_type=jnp.float32
        )
        for part in (keep_rows, send_rows)
    ]
    up_grad = reduce_scatter_halving(keep_term, send_term, "dp", RS_ORDER, RS_TWIN)
    return (caption_loss, image_grad, up_grad, down_grad)


def solution(mesh):
    in_specs = (P("dp", None), P("dp"), P("dp", None), P(), P(None, "mp"), P(None, "mp"))
    out_specs = (P("dp"), P("dp", None), P("dp", "mp"), P("dp", "mp"))
    return jax.shard_map(
        on_device, mesh=mesh, in_specs=in_specs, out_specs=out_specs, check_vma=False
    )
```

```python
import jax
import jax.numpy as jnp
from jax import lax
from jax.sharding import PartitionSpec as P

LOGIT_SCALE = 117.0
LOGIT_SHIFT = -12.9
RS_ORDER = (0, 3, 1, 4, 2, 5)
RS_TWIN = (0, 4, 3, 1, 5, 2)


def passed_along(value, axis, steps):
    count = lax.axis_size(axis)
    pairs = [(source, (source + steps) % count) for source in range(count)]
    return lax.ppermute(value, axis, pairs)


def layer_norm(rows):
    center = rows - jnp.mean(rows, -1, keepdims=True)
    spread = jnp.mean(center * center, -1, keepdims=True)
    return center * lax.rsqrt(spread + 1e-06)


def gelu_pair(pre):
    const = 0.7978845608028654
    inner = const * (pre + 0.044715 * pre * pre * pre)
    tanh_u = jnp.tanh(inner)
    value = 0.5 * pre * (1.0 + tanh_u)
    slope = 0.5 * (1.0 + tanh_u) + 0.5 * pre * (1.0 - tanh_u * tanh_u) * const * (
        1.0 + 3.0 * 0.044715 * pre * pre
    )
    return (value, slope)


def unit_rows(rows):
    scale = lax.rsqrt(jnp.sum(rows * rows, 1, keepdims=True) + 1e-06)
    return (rows * scale, scale)


def pair_coef(own_rows, own_group, other_rows, other_group):
    logits = (
        LOGIT_SCALE
        * lax.dot_general(
            own_rows, other_rows, (((1,), (1,)), ((), ())), preferred_element_type=jnp.float32
        )
        + LOGIT_SHIFT
    )
    signs = jnp.where(own_group[:, None] == other_group[None, :], 1.0, -1.0).astype(jnp.float32)
    coef = (-LOGIT_SCALE * signs * jax.nn.sigmoid(-signs * logits)).astype(jnp.bfloat16)
    return (logits, signs, coef)


def permuted_blocks(blocks, depth, first, second):
    lead = blocks.shape[:1]
    swap = dict(zip(first, second))
    split = blocks.reshape(lead + (2,) * depth + blocks.shape[2:])
    moved = [1 + depth - 1 - swap[depth - 1 - place] for place in range(depth)]
    axes = [0] + moved + list(range(1 + depth, split.ndim))
    return jnp.transpose(split, axes).reshape(blocks.shape)


def first_stage_halves(natural, permuted, variant):
    shape = natural.shape
    halves = shape[:1] + (shape[1] // 2, 2) + shape[2:]
    own = jnp.where(variant == 0, natural, permuted).reshape(halves)
    other = jnp.where(variant == 0, permuted, natural).reshape(halves)
    keep = lax.dynamic_index_in_dim(own, variant, axis=2, keepdims=False)
    send = lax.dynamic_index_in_dim(other, 1 - variant, axis=2, keepdims=False)
    return (keep, send)


def reduce_scatter_halving(keep, send, axis, first, second):
    devices = lax.axis_size(axis)
    own_index = lax.axis_index(axis)
    depth = devices.bit_length() - 1
    pairs = [(source, source ^ 1) for source in range(devices)]
    state = keep + lax.ppermute(send, axis, pairs)
    left = list(range(depth - 1, 0, -1))
    state = state.reshape((2,) * (depth - 1) + state.shape[1:])
    variant = own_index & 1
    for bit, twin in zip(first[1:], second[1:]):
        place = left.index(bit)
        own_bit = jnp.where(variant == 0, (own_index >> bit) & 1, (own_index >> twin) & 1)
        keep = lax.dynamic_index_in_dim(state, own_bit, axis=place, keepdims=False)
        send = lax.dynamic_index_in_dim(state, 1 - own_bit, axis=place, keepdims=False)
        pairs = [
            (source, source ^ (1 << (bit if source & 1 == 0 else twin)))
            for source in range(devices)
        ]
        state = keep + lax.ppermute(send, axis, pairs)
        left.remove(bit)
    return state


def all_gather_doubling(block, axis, order):
    devices = lax.axis_size(axis)
    own_index = lax.axis_index(axis)
    depth = devices.bit_length() - 1
    state = block[None]
    gathered = []
    for bit in order:
        place = sum(1 for done in gathered if done > bit)
        pairs = [(source, source ^ (1 << bit)) for source in range(devices)]
        other = lax.ppermute(state, axis, pairs)
        low_first = jnp.stack([state, other], axis=place)
        high_first = jnp.stack([other, state], axis=place)
        state = jnp.where(((own_index >> bit) & 1) == 0, low_first, high_first)
        gathered.append(bit)
    return state.reshape((devices * block.shape[0],) + block.shape[1:])


def on_device(tokens, lengths, images, pair_group, w_up, w_down):
    captions = lengths.shape[0]
    seq_len = tokens.shape[0] // captions
    width = tokens.shape[1]
    hidden = w_up.shape[1]
    devices = lax.axis_size("dp")
    own_index = lax.axis_index("dp")
    total = captions * devices
    rows = width // devices
    own_group = lax.dynamic_slice_in_dim(pair_group, own_index * captions, captions)

    unit_image, image_scale = unit_rows(images.astype(jnp.float32))
    image_half = unit_image.astype(jnp.bfloat16)

    tok_float = tokens.astype(jnp.float32)
    normed = layer_norm(tok_float).astype(jnp.bfloat16)
    pre = jnp.dot(normed, w_up, preferred_element_type=jnp.float32)
    value, slope = gelu_pair(pre)
    position = jnp.arange(seq_len, dtype=jnp.int32)
    valid = (position[None, :] < lengths[:, None]).astype(jnp.float32)
    share = valid / jnp.sum(valid, 1, keepdims=True)
    owner = jnp.arange(captions * seq_len, dtype=jnp.int32) // seq_len
    share_rows = jnp.where(
        owner[None, :] == jnp.arange(captions, dtype=jnp.int32)[:, None],
        share.reshape(1, captions * seq_len),
        0.0,
    )
    gmean = jnp.dot(
        share_rows, value, precision=lax.Precision.HIGHEST, preferred_element_type=jnp.float32
    )
    tmean = jnp.sum(tok_float.reshape(captions, seq_len, width) * share[:, :, None], 1)
    gbar = gmean.astype(jnp.bfloat16)
    gbar_all = lax.all_gather(gbar, "dp", tiled=True)
    partial_value = lax.dot_general(
        gbar, w_down, (((1,), (1,)), ((), ())), preferred_element_type=jnp.float32
    )
    pooled = tmean + (partial_value + passed_along(partial_value, "mp", 1))
    unit_text, text_scale = unit_rows(pooled)
    text_half = unit_text.astype(jnp.bfloat16)
    both_all = all_gather_doubling(
        jnp.concatenate([text_half, image_half], 1), "dp", RS_ORDER[::-1]
    )
    text_all = both_all[:, :width]
    image_all = both_all[:, width:]

    logits, signs, coef = pair_coef(text_half, own_group, image_all, pair_group)
    caption_loss = -jnp.sum(jax.nn.log_sigmoid(signs * logits), 1) / total
    text_back = jnp.dot(coef, image_all, preferred_element_type=jnp.float32)
    _, _, coef_cols = pair_coef(image_half, own_group, text_all, pair_group)
    img_back = jnp.dot(coef_cols, text_all, preferred_element_type=jnp.float32)

    pooled_grad = (
        text_back - unit_text * jnp.sum(unit_text * text_back, 1, keepdims=True)
    ) * text_scale
    image_grad = (
        img_back - unit_image * jnp.sum(unit_image * img_back, 1, keepdims=True)
    ) * image_scale
    pooled_half = pooled_grad.astype(jnp.bfloat16)
    pooled_rows = lax.all_to_all(
        pooled_half.reshape(captions, devices, rows), "dp", 1, 0
    ).reshape(total, rows)
    down_grad = lax.dot_general(
        pooled_rows, gbar_all, (((0,), (0,)), ((), ())), preferred_element_type=jnp.float32
    )
    hidden_grad = jnp.dot(pooled_half, w_down, preferred_element_type=jnp.float32)
    spread_grad = lax.dot_general(
        share_rows,
        hidden_grad,
        (((0,), (0,)), ((), ())),
        precision=lax.Precision.HIGHEST,
        preferred_element_type=jnp.float32,
    )
    pre_grad = (spread_grad * slope).astype(jnp.bfloat16)
    normed_blocks = normed.reshape(captions * seq_len, devices, rows)
    depth = devices.bit_length() - 1
    keep_rows, send_rows = first_stage_halves(
        normed_blocks,
        permuted_blocks(normed_blocks, depth, RS_ORDER, RS_TWIN),
        own_index & 1,
    )
    keep_term, send_term = [
        lax.dot_general(
            part, pre_grad, (((0,), (0,)), ((), ())), preferred_element_type=jnp.float32
        )
        for part in (keep_rows, send_rows)
    ]
    up_grad = reduce_scatter_halving(keep_term, send_term, "dp", RS_ORDER, RS_TWIN)
    return (caption_loss, image_grad, up_grad, down_grad)


def solution(mesh):
    in_specs = (P("dp", None), P("dp"), P("dp", None), P(), P(None, "mp"), P(None, "mp"))
    out_specs = (P("dp"), P("dp", None), P("dp", "mp"), P("dp", "mp"))
    return jax.shard_map(
        on_device, mesh=mesh, in_specs=in_specs, out_specs=out_specs, check_vma=False
    )
```

```python
import jax
import jax.numpy as jnp
from jax import lax
from jax.sharding import PartitionSpec as P

LOGIT_SCALE = 117.0
LOGIT_SHIFT = -12.9
RS_ORDER = (0, 3, 1, 4, 2, 5)
RS_TWIN = (0, 4, 3, 1, 5, 2)


def passed_along(value, axis, steps):
    count = lax.axis_size(axis)
    pairs = [(source, (source + steps) % count) for source in range(count)]
    return lax.ppermute(value, axis, pairs)


def layer_norm(rows):
    center = rows - jnp.mean(rows, -1, keepdims=True)
    spread = jnp.mean(center * center, -1, keepdims=True)
    return center * lax.rsqrt(spread + 1e-06)


def gelu_pair(pre):
    const = 0.7978845608028654
    inner = const * (pre + 0.044715 * pre * pre * pre)
    tanh_u = jnp.tanh(inner)
    value = 0.5 * pre * (1.0 + tanh_u)
    slope = 0.5 * (1.0 + tanh_u) + 0.5 * pre * (1.0 - tanh_u * tanh_u) * const * (
        1.0 + 3.0 * 0.044715 * pre * pre
    )
    return (value, slope)


def unit_rows(rows):
    scale = lax.rsqrt(jnp.sum(rows * rows, 1, keepdims=True) + 1e-06)
    return (rows * scale, scale)


def pair_coef(own_rows, own_group, other_rows, other_group):
    logits = (
        LOGIT_SCALE
        * lax.dot_general(
            own_rows, other_rows, (((1,), (1,)), ((), ())), preferred_element_type=jnp.float32
        )
        + LOGIT_SHIFT
    )
    signs = jnp.where(own_group[:, None] == other_group[None, :], 1.0, -1.0).astype(jnp.float32)
    coef = (-LOGIT_SCALE * signs * jax.nn.sigmoid(-signs * logits)).astype(jnp.bfloat16)
    return (logits, signs, coef)


def permuted_blocks(blocks, depth, first, second):
    lead = blocks.shape[:1]
    swap = dict(zip(first, second))
    split = blocks.reshape(lead + (2,) * depth + blocks.shape[2:])
    moved = [1 + depth - 1 - swap[depth - 1 - place] for place in range(depth)]
    axes = [0] + moved + list(range(1 + depth, split.ndim))
    return jnp.transpose(split, axes).reshape(blocks.shape)


def first_stage_halves(natural, permuted, variant):
    shape = natural.shape
    halves = shape[:1] + (shape[1] // 2, 2) + shape[2:]
    own = jnp.where(variant == 0, natural, permuted).reshape(halves)
    other = jnp.where(variant == 0, permuted, natural).reshape(halves)
    keep = lax.dynamic_index_in_dim(own, variant, axis=2, keepdims=False)
    send = lax.dynamic_index_in_dim(other, 1 - variant, axis=2, keepdims=False)
    return (keep, send)


def reduce_scatter_halving(keep, send, axis, first, second):
    devices = lax.axis_size(axis)
    own_index = lax.axis_index(axis)
    depth = devices.bit_length() - 1
    pairs = [(source, source ^ 1) for source in range(devices)]
    state = keep + lax.ppermute(send, axis, pairs)
    left = list(range(depth - 1, 0, -1))
    state = state.reshape((2,) * (depth - 1) + state.shape[1:])
    variant = own_index & 1
    for bit, twin in zip(first[1:], second[1:]):
        place = left.index(bit)
        own_bit = jnp.where(variant == 0, (own_index >> bit) & 1, (own_index >> twin) & 1)
        keep = lax.dynamic_index_in_dim(state, own_bit, axis=place, keepdims=False)
        send = lax.dynamic_index_in_dim(state, 1 - own_bit, axis=place, keepdims=False)
        pairs = [
            (source, source ^ (1 << (bit if source & 1 == 0 else twin)))
            for source in range(devices)
        ]
        state = keep + lax.ppermute(send, axis, pairs)
        left.remove(bit)
    return state


def all_gather_doubling(block, axis, first, second):
    devices = lax.axis_size(axis)
    own_index = lax.axis_index(axis)
    variant = own_index & 1
    state = block[None]
    gathered = []
    for bit, twin in zip(first[:-1], second[:-1]):
        place = sum(1 for done in gathered if done > bit)
        pairs = [
            (source, source ^ (1 << (bit if source & 1 == 0 else twin)))
            for source in range(devices)
        ]
        other = lax.ppermute(state, axis, pairs)
        low_first = jnp.stack([state, other], axis=place)
        high_first = jnp.stack([other, state], axis=place)
        own_bit = jnp.where(variant == 0, (own_index >> bit) & 1, (own_index >> twin) & 1)
        state = jnp.where(own_bit == 0, low_first, high_first)
        gathered.append(bit)
    labels = sorted(gathered, reverse=True)
    holds = dict(zip(first[:-1], second[:-1]))
    source_of = {holds[label]: label for label in labels}
    axes = [labels.index(source_of[label]) for label in labels]
    axes = axes + list(range(len(labels), state.ndim))
    state = jnp.where(variant == 0, state, jnp.transpose(state, axes))
    last = first[-1]
    pairs = [(source, source ^ (1 << last)) for source in range(devices)]
    other = lax.ppermute(state, axis, pairs)
    place = sum(1 for done in gathered if done > last)
    low_first = jnp.stack([state, other], axis=place)
    high_first = jnp.stack([other, state], axis=place)
    state = jnp.where(((own_index >> last) & 1) == 0, low_first, high_first)
    return state.reshape((devices * block.shape[0],) + block.shape[1:])


def on_device(tokens, lengths, images, pair_group, w_up, w_down):
    captions = lengths.shape[0]
    seq_len = tokens.shape[0] // captions
    width = tokens.shape[1]
    hidden = w_up.shape[1]
    devices = lax.axis_size("dp")
    own_index = lax.axis_index("dp")
    total = captions * devices
    rows = width // devices
    own_group = lax.dynamic_slice_in_dim(pair_group, own_index * captions, captions)

    unit_image, image_scale = unit_rows(images.astype(jnp.float32))
    image_half = unit_image.astype(jnp.bfloat16)

    tok_float = tokens.astype(jnp.float32)
    normed = layer_norm(tok_float).astype(jnp.bfloat16)
    pre = jnp.dot(normed, w_up, preferred_element_type=jnp.float32)
    value, slope = gelu_pair(pre)
    position = jnp.arange(seq_len, dtype=jnp.int32)
    valid = (position[None, :] < lengths[:, None]).astype(jnp.float32)
    share = valid / jnp.sum(valid, 1, keepdims=True)
    owner = jnp.arange(captions * seq_len, dtype=jnp.int32) // seq_len
    share_rows = jnp.where(
        owner[None, :] == jnp.arange(captions, dtype=jnp.int32)[:, None],
        share.reshape(1, captions * seq_len),
        0.0,
    )
    gmean = jnp.dot(
        share_rows, value, precision=lax.Precision.HIGHEST, preferred_element_type=jnp.float32
    )
    tmean = jnp.sum(tok_float.reshape(captions, seq_len, width) * share[:, :, None], 1)
    gbar = gmean.astype(jnp.bfloat16)
    gbar_all = lax.all_gather(gbar, "dp", tiled=True)
    partial_value = lax.dot_general(
        gbar, w_down, (((1,), (1,)), ((), ())), preferred_element_type=jnp.float32
    )
    pooled = tmean + (partial_value + passed_along(partial_value, "mp", 1))
    unit_text, text_scale = unit_rows(pooled)
    text_half = unit_text.astype(jnp.bfloat16)
    both_all = all_gather_doubling(
        jnp.concatenate([text_half, image_half], 1), "dp", RS_ORDER[::-1], RS_TWIN[::-1]
    )
    text_all = both_all[:, :width]
    image_all = both_all[:, width:]

    logits, signs, coef = pair_coef(text_half, own_group, image_all, pair_group)
    caption_loss = -jnp.sum(jax.nn.log_sigmoid(signs * logits), 1) / total
    text_back = jnp.dot(coef, image_all, preferred_element_type=jnp.float32)
    _, _, coef_cols = pair_coef(image_half, own_group, text_all, pair_group)
    img_back = jnp.dot(coef_cols, text_all, preferred_element_type=jnp.float32)

    pooled_grad = (
        text_back - unit_text * jnp.sum(unit_text * text_back, 1, keepdims=True)
    ) * text_scale
    image_grad = (
        img_back - unit_image * jnp.sum(unit_image * img_back, 1, keepdims=True)
    ) * image_scale
    pooled_half = pooled_grad.astype(jnp.bfloat16)
    pooled_rows = lax.all_to_all(
        pooled_half.reshape(captions, devices, rows), "dp", 1, 0
    ).reshape(total, rows)
    down_grad = lax.dot_general(
        pooled_rows, gbar_all, (((0,), (0,)), ((), ())), preferred_element_type=jnp.float32
    )
    hidden_grad = jnp.dot(pooled_half, w_down, preferred_element_type=jnp.float32)
    spread_grad = lax.dot_general(
        share_rows,
        hidden_grad,
        (((0,), (0,)), ((), ())),
        precision=lax.Precision.HIGHEST,
        preferred_element_type=jnp.float32,
    )
    pre_grad = (spread_grad * slope).astype(jnp.bfloat16)
    normed_blocks = normed.reshape(captions * seq_len, devices, rows)
    depth = devices.bit_length() - 1
    keep_rows, send_rows = first_stage_halves(
        normed_blocks,
        permuted_blocks(normed_blocks, depth, RS_ORDER, RS_TWIN),
        own_index & 1,
    )
    keep_term, send_term = [
        lax.dot_general(
            part, pre_grad, (((0,), (0,)), ((), ())), preferred_element_type=jnp.float32
        )
        for part in (keep_rows, send_rows)
    ]
    up_grad = reduce_scatter_halving(keep_term, send_term, "dp", RS_ORDER, RS_TWIN)
    return (caption_loss, image_grad, up_grad, down_grad)


def solution(mesh):
    in_specs = (P("dp", None), P("dp"), P("dp", None), P(), P(None, "mp"), P(None, "mp"))
    out_specs = (P("dp"), P("dp", None), P("dp", "mp"), P("dp", "mp"))
    return jax.shard_map(
        on_device, mesh=mesh, in_specs=in_specs, out_specs=out_specs, check_vma=False
    )
```

```python
import jax
import jax.numpy as jnp
from jax import lax
from jax.sharding import PartitionSpec as P

LOGIT_SCALE = 117.0
LOGIT_SHIFT = -12.9
RS_ORDER = (0, 3, 1, 4, 2, 5)
RS_TWIN = (0, 4, 3, 1, 5, 2)


def passed_along(value, axis, steps):
    count = lax.axis_size(axis)
    pairs = [(source, (source + steps) % count) for source in range(count)]
    return lax.ppermute(value, axis, pairs)


def layer_norm(rows):
    center = rows - jnp.mean(rows, -1, keepdims=True)
    spread = jnp.mean(center * center, -1, keepdims=True)
    return center * lax.rsqrt(spread + 1e-06)


def gelu_pair(pre):
    const = 0.7978845608028654
    inner = const * (pre + 0.044715 * pre * pre * pre)
    tanh_u = jnp.tanh(inner)
    value = 0.5 * pre * (1.0 + tanh_u)
    slope = 0.5 * (1.0 + tanh_u) + 0.5 * pre * (1.0 - tanh_u * tanh_u) * const * (
        1.0 + 3.0 * 0.044715 * pre * pre
    )
    return (value, slope)


def unit_rows(rows):
    scale = lax.rsqrt(jnp.sum(rows * rows, 1, keepdims=True) + 1e-06)
    return (rows * scale, scale)


def pair_coef(own_rows, own_group, other_rows, other_group):
    logits = (
        LOGIT_SCALE
        * lax.dot_general(
            own_rows, other_rows, (((1,), (1,)), ((), ())), preferred_element_type=jnp.float32
        )
        + LOGIT_SHIFT
    )
    signs = jnp.where(own_group[:, None] == other_group[None, :], 1.0, -1.0).astype(jnp.float32)
    coef = (-LOGIT_SCALE * signs * jax.nn.sigmoid(-signs * logits)).astype(jnp.bfloat16)
    return (logits, signs, coef)


def permuted_blocks(blocks, depth, first, second):
    lead = blocks.shape[:1]
    swap = dict(zip(first, second))
    split = blocks.reshape(lead + (2,) * depth + blocks.shape[2:])
    moved = [1 + depth - 1 - swap[depth - 1 - place] for place in range(depth)]
    axes = [0] + moved + list(range(1 + depth, split.ndim))
    return jnp.transpose(split, axes).reshape(blocks.shape)


def first_stage_halves(natural, permuted, variant):
    shape = natural.shape
    halves = shape[:1] + (shape[1] // 2, 2) + shape[2:]
    own = jnp.where(variant == 0, natural, permuted).reshape(halves)
    other = jnp.where(variant == 0, permuted, natural).reshape(halves)
    keep = lax.dynamic_index_in_dim(own, variant, axis=2, keepdims=False)
    send = lax.dynamic_index_in_dim(other, 1 - variant, axis=2, keepdims=False)
    return (keep, send)


def reduce_scatter_halving(keep, send, axis, first, second):
    devices = lax.axis_size(axis)
    own_index = lax.axis_index(axis)
    depth = devices.bit_length() - 1
    pairs = [(source, source ^ 1) for source in range(devices)]
    state = keep + lax.ppermute(send, axis, pairs)
    left = list(range(depth - 1, 0, -1))
    state = state.reshape((2,) * (depth - 1) + state.shape[1:])
    variant = own_index & 1
    for bit, twin in zip(first[1:], second[1:]):
        place = left.index(bit)
        own_bit = jnp.where(variant == 0, (own_index >> bit) & 1, (own_index >> twin) & 1)
        keep = lax.dynamic_index_in_dim(state, own_bit, axis=place, keepdims=False)
        send = lax.dynamic_index_in_dim(state, 1 - own_bit, axis=place, keepdims=False)
        pairs = [
            (source, source ^ (1 << (bit if source & 1 == 0 else twin)))
            for source in range(devices)
        ]
        state = keep + lax.ppermute(send, axis, pairs)
        left.remove(bit)
    return state


def all_gather_doubling(block, axis, order, companion=None, tie_at=0):
    devices = lax.axis_size(axis)
    own_index = lax.axis_index(axis)
    depth = devices.bit_length() - 1
    state = block[None]
    gathered = []
    for step, bit in enumerate(order):
        place = sum(1 for done in gathered if done > bit)
        pairs = [(source, source ^ (1 << bit)) for source in range(devices)]
        other = lax.ppermute(state, axis, pairs)
        if step == tie_at and companion is not None:
            other, companion = lax.optimization_barrier((other, companion))
        low_first = jnp.stack([state, other], axis=place)
        high_first = jnp.stack([other, state], axis=place)
        state = jnp.where(((own_index >> bit) & 1) == 0, low_first, high_first)
        gathered.append(bit)
    return (state.reshape((devices * block.shape[0],) + block.shape[1:]), companion)


def on_device(tokens, lengths, images, pair_group, w_up, w_down):
    captions = lengths.shape[0]
    seq_len = tokens.shape[0] // captions
    width = tokens.shape[1]
    hidden = w_up.shape[1]
    devices = lax.axis_size("dp")
    own_index = lax.axis_index("dp")
    total = captions * devices
    rows = width // devices
    own_group = lax.dynamic_slice_in_dim(pair_group, own_index * captions, captions)

    unit_image, image_scale = unit_rows(images.astype(jnp.float32))
    image_half = unit_image.astype(jnp.bfloat16)

    tok_float = tokens.astype(jnp.float32)
    normed = layer_norm(tok_float).astype(jnp.bfloat16)
    pre = jnp.dot(normed, w_up, preferred_element_type=jnp.float32)
    value, slope = gelu_pair(pre)
    position = jnp.arange(seq_len, dtype=jnp.int32)
    valid = (position[None, :] < lengths[:, None]).astype(jnp.float32)
    share = valid / jnp.sum(valid, 1, keepdims=True)
    owner = jnp.arange(captions * seq_len, dtype=jnp.int32) // seq_len
    share_rows = jnp.where(
        owner[None, :] == jnp.arange(captions, dtype=jnp.int32)[:, None],
        share.reshape(1, captions * seq_len),
        0.0,
    )
    gmean = jnp.dot(
        share_rows, value, precision=lax.Precision.HIGHEST, preferred_element_type=jnp.float32
    )
    tmean = jnp.sum(tok_float.reshape(captions, seq_len, width) * share[:, :, None], 1)
    gbar = gmean.astype(jnp.bfloat16)
    gbar_all = lax.all_gather(gbar, "dp", tiled=True)
    partial_value = lax.dot_general(
        gbar, w_down, (((1,), (1,)), ((), ())), preferred_element_type=jnp.float32
    )
    pooled = tmean + (partial_value + passed_along(partial_value, "mp", 1))
    unit_text, text_scale = unit_rows(pooled)
    text_half = unit_text.astype(jnp.bfloat16)
    normed_blocks = normed.reshape(captions * seq_len, devices, rows)
    depth = devices.bit_length() - 1
    keep_rows, send_rows = first_stage_halves(
        normed_blocks,
        permuted_blocks(normed_blocks, depth, RS_ORDER, RS_TWIN),
        own_index & 1,
    )
    both_all, (keep_rows, send_rows) = all_gather_doubling(
        jnp.concatenate([text_half, image_half], 1),
        "dp",
        RS_ORDER[::-1],
        (keep_rows, send_rows),
        len(RS_ORDER) - 2,
    )
    text_all = both_all[:, :width]
    image_all = both_all[:, width:]

    logits, signs, coef = pair_coef(text_half, own_group, image_all, pair_group)
    caption_loss = -jnp.sum(jax.nn.log_sigmoid(signs * logits), 1) / total
    text_back = jnp.dot(coef, image_all, preferred_element_type=jnp.float32)
    _, _, coef_cols = pair_coef(image_half, own_group, text_all, pair_group)
    img_back = jnp.dot(coef_cols, text_all, preferred_element_type=jnp.float32)

    pooled_grad = (
        text_back - unit_text * jnp.sum(unit_text * text_back, 1, keepdims=True)
    ) * text_scale
    image_grad = (
        img_back - unit_image * jnp.sum(unit_image * img_back, 1, keepdims=True)
    ) * image_scale
    pooled_half = pooled_grad.astype(jnp.bfloat16)
    pooled_rows = lax.all_to_all(
        pooled_half.reshape(captions, devices, rows), "dp", 1, 0
    ).reshape(total, rows)
    down_grad = lax.dot_general(
        pooled_rows, gbar_all, (((0,), (0,)), ((), ())), preferred_element_type=jnp.float32
    )
    hidden_grad = jnp.dot(pooled_half, w_down, preferred_element_type=jnp.float32)
    spread_grad = lax.dot_general(
        share_rows,
        hidden_grad,
        (((0,), (0,)), ((), ())),
        precision=lax.Precision.HIGHEST,
        preferred_element_type=jnp.float32,
    )
    pre_grad = (spread_grad * slope).astype(jnp.bfloat16)
    keep_term, send_term = [
        lax.dot_general(
            part, pre_grad, (((0,), (0,)), ((), ())), preferred_element_type=jnp.float32
        )
        for part in (keep_rows, send_rows)
    ]
    up_grad = reduce_scatter_halving(keep_term, send_term, "dp", RS_ORDER, RS_TWIN)
    return (caption_loss, image_grad, up_grad, down_grad)


def solution(mesh):
    in_specs = (P("dp", None), P("dp"), P("dp", None), P(), P(None, "mp"), P(None, "mp"))
    out_specs = (P("dp"), P("dp", None), P("dp", "mp"), P("dp", "mp"))
    return jax.shard_map(
        on_device, mesh=mesh, in_specs=in_specs, out_specs=out_specs, check_vma=False
    )
```

```python
import jax
import jax.numpy as jnp
from jax import lax
from jax.sharding import PartitionSpec as P

LOGIT_SCALE = 117.0
LOGIT_SHIFT = -12.9
RS_ORDER = (0, 3, 1, 4, 2, 5)
RS_TWIN = (0, 4, 3, 1, 5, 2)


def passed_along(value, axis, steps):
    count = lax.axis_size(axis)
    pairs = [(source, (source + steps) % count) for source in range(count)]
    return lax.ppermute(value, axis, pairs)


def layer_norm(rows):
    center = rows - jnp.mean(rows, -1, keepdims=True)
    spread = jnp.mean(center * center, -1, keepdims=True)
    return center * lax.rsqrt(spread + 1e-06)


def gelu_pair(pre):
    const = 0.7978845608028654
    inner = const * (pre + 0.044715 * pre * pre * pre)
    tanh_u = jnp.tanh(inner)
    value = 0.5 * pre * (1.0 + tanh_u)
    slope = 0.5 * (1.0 + tanh_u) + 0.5 * pre * (1.0 - tanh_u * tanh_u) * const * (
        1.0 + 3.0 * 0.044715 * pre * pre
    )
    return (value, slope)


def unit_rows(rows):
    scale = lax.rsqrt(jnp.sum(rows * rows, 1, keepdims=True) + 1e-06)
    return (rows * scale, scale)


def pair_coef(own_rows, own_group, other_rows, other_group):
    logits = (
        LOGIT_SCALE
        * lax.dot_general(
            own_rows, other_rows, (((1,), (1,)), ((), ())), preferred_element_type=jnp.float32
        )
        + LOGIT_SHIFT
    )
    signs = jnp.where(own_group[:, None] == other_group[None, :], 1.0, -1.0).astype(jnp.float32)
    coef = (-LOGIT_SCALE * signs * jax.nn.sigmoid(-signs * logits)).astype(jnp.bfloat16)
    return (logits, signs, coef)


def permuted_blocks(blocks, depth, first, second):
    lead = blocks.shape[:1]
    swap = dict(zip(first, second))
    split = blocks.reshape(lead + (2,) * depth + blocks.shape[2:])
    moved = [1 + depth - 1 - swap[depth - 1 - place] for place in range(depth)]
    axes = [0] + moved + list(range(1 + depth, split.ndim))
    return jnp.transpose(split, axes).reshape(blocks.shape)


def first_stage_halves(natural, permuted, variant):
    shape = natural.shape
    halves = shape[:1] + (shape[1] // 2, 2) + shape[2:]
    own = jnp.where(variant == 0, natural, permuted).reshape(halves)
    other = jnp.where(variant == 0, permuted, natural).reshape(halves)
    keep = lax.dynamic_index_in_dim(own, variant, axis=2, keepdims=False)
    send = lax.dynamic_index_in_dim(other, 1 - variant, axis=2, keepdims=False)
    return (keep, send)


def reduce_scatter_halving(keep, send, axis, first, second):
    devices = lax.axis_size(axis)
    own_index = lax.axis_index(axis)
    depth = devices.bit_length() - 1
    pairs = [(source, source ^ 1) for source in range(devices)]
    state = keep + lax.ppermute(send, axis, pairs)
    left = list(range(depth - 1, 0, -1))
    state = state.reshape((2,) * (depth - 1) + state.shape[1:])
    variant = own_index & 1
    for bit, twin in zip(first[1:], second[1:]):
        place = left.index(bit)
        own_bit = jnp.where(variant == 0, (own_index >> bit) & 1, (own_index >> twin) & 1)
        keep = lax.dynamic_index_in_dim(state, own_bit, axis=place, keepdims=False)
        send = lax.dynamic_index_in_dim(state, 1 - own_bit, axis=place, keepdims=False)
        pairs = [
            (source, source ^ (1 << (bit if source & 1 == 0 else twin)))
            for source in range(devices)
        ]
        state = keep + lax.ppermute(send, axis, pairs)
        left.remove(bit)
    return state


def all_gather_doubling(block, axis, order, companion=None, tie_at=0):
    devices = lax.axis_size(axis)
    own_index = lax.axis_index(axis)
    depth = devices.bit_length() - 1
    state = block[None]
    gathered = []
    for step, bit in enumerate(order):
        place = sum(1 for done in gathered if done > bit)
        pairs = [(source, source ^ (1 << bit)) for source in range(devices)]
        other = lax.ppermute(state, axis, pairs)
        if step == tie_at and companion is not None:
            other, companion = lax.optimization_barrier((other, companion))
        low_first = jnp.stack([state, other], axis=place)
        high_first = jnp.stack([other, state], axis=place)
        state = jnp.where(((own_index >> bit) & 1) == 0, low_first, high_first)
        gathered.append(bit)
    return (state.reshape((devices * block.shape[0],) + block.shape[1:]), companion)


def on_device(tokens, lengths, images, pair_group, w_up, w_down):
    captions = lengths.shape[0]
    seq_len = tokens.shape[0] // captions
    width = tokens.shape[1]
    hidden = w_up.shape[1]
    devices = lax.axis_size("dp")
    own_index = lax.axis_index("dp")
    total = captions * devices
    rows = width // devices
    own_group = lax.dynamic_slice_in_dim(pair_group, own_index * captions, captions)

    unit_image, image_scale = unit_rows(images.astype(jnp.float32))
    image_half = unit_image.astype(jnp.bfloat16)

    tok_float = tokens.astype(jnp.float32)
    normed = layer_norm(tok_float).astype(jnp.bfloat16)
    pre = jnp.dot(normed, w_up, preferred_element_type=jnp.float32)
    value, slope = gelu_pair(pre)
    position = jnp.arange(seq_len, dtype=jnp.int32)
    valid = (position[None, :] < lengths[:, None]).astype(jnp.float32)
    share = valid / jnp.sum(valid, 1, keepdims=True)
    owner = jnp.arange(captions * seq_len, dtype=jnp.int32) // seq_len
    share_rows = jnp.where(
        owner[None, :] == jnp.arange(captions, dtype=jnp.int32)[:, None],
        share.reshape(1, captions * seq_len),
        0.0,
    )
    gmean = jnp.dot(
        share_rows, value, precision=lax.Precision.HIGHEST, preferred_element_type=jnp.float32
    )
    tmean = jnp.sum(tok_float.reshape(captions, seq_len, width) * share[:, :, None], 1)
    gbar = gmean.astype(jnp.bfloat16)
    gbar_all, _ = all_gather_doubling(gbar, "dp", RS_TWIN[::-1])
    partial_value = lax.dot_general(
        gbar, w_down, (((1,), (1,)), ((), ())), preferred_element_type=jnp.float32
    )
    pooled = tmean + (partial_value + passed_along(partial_value, "mp", 1))
    unit_text, text_scale = unit_rows(pooled)
    text_half = unit_text.astype(jnp.bfloat16)
    normed_blocks = normed.reshape(captions * seq_len, devices, rows)
    depth = devices.bit_length() - 1
    keep_rows, send_rows = first_stage_halves(
        normed_blocks,
        permuted_blocks(normed_blocks, depth, RS_ORDER, RS_TWIN),
        own_index & 1,
    )
    both_all, (keep_rows, send_rows) = all_gather_doubling(
        jnp.concatenate([text_half, image_half], 1),
        "dp",
        RS_ORDER[::-1],
        (keep_rows, send_rows),
        len(RS_ORDER) - 2,
    )
    text_all = both_all[:, :width]
    image_all = both_all[:, width:]

    logits, signs, coef = pair_coef(text_half, own_group, image_all, pair_group)
    caption_loss = -jnp.sum(jax.nn.log_sigmoid(signs * logits), 1) / total
    text_back = jnp.dot(coef, image_all, preferred_element_type=jnp.float32)
    _, _, coef_cols = pair_coef(image_half, own_group, text_all, pair_group)
    img_back = jnp.dot(coef_cols, text_all, preferred_element_type=jnp.float32)

    pooled_grad = (
        text_back - unit_text * jnp.sum(unit_text * text_back, 1, keepdims=True)
    ) * text_scale
    image_grad = (
        img_back - unit_image * jnp.sum(unit_image * img_back, 1, keepdims=True)
    ) * image_scale
    pooled_half = pooled_grad.astype(jnp.bfloat16)
    pooled_rows = lax.all_to_all(
        pooled_half.reshape(captions, devices, rows), "dp", 1, 0
    ).reshape(total, rows)
    down_grad = lax.dot_general(
        pooled_rows, gbar_all, (((0,), (0,)), ((), ())), preferred_element_type=jnp.float32
    )
    hidden_grad = jnp.dot(pooled_half, w_down, preferred_element_type=jnp.float32)
    spread_grad = lax.dot_general(
        share_rows,
        hidden_grad,
        (((0,), (0,)), ((), ())),
        precision=lax.Precision.HIGHEST,
        preferred_element_type=jnp.float32,
    )
    pre_grad = (spread_grad * slope).astype(jnp.bfloat16)
    keep_term, send_term = [
        lax.dot_general(
            part, pre_grad, (((0,), (0,)), ((), ())), preferred_element_type=jnp.float32
        )
        for part in (keep_rows, send_rows)
    ]
    up_grad = reduce_scatter_halving(keep_term, send_term, "dp", RS_ORDER, RS_TWIN)
    return (caption_loss, image_grad, up_grad, down_grad)


def solution(mesh):
    in_specs = (P("dp", None), P("dp"), P("dp", None), P(), P(None, "mp"), P(None, "mp"))
    out_specs = (P("dp"), P("dp", None), P("dp", "mp"), P("dp", "mp"))
    return jax.shard_map(
        on_device, mesh=mesh, in_specs=in_specs, out_specs=out_specs, check_vma=False
    )
```

```python
import jax
import jax.numpy as jnp
from jax import lax
from jax.sharding import PartitionSpec as P

LOGIT_SCALE = 117.0
LOGIT_SHIFT = -12.9
RS_ORDER = (0, 3, 1, 4, 2, 5)
RS_TWIN = (0, 4, 3, 1, 5, 2)


def passed_along(value, axis, steps):
    count = lax.axis_size(axis)
    pairs = [(source, (source + steps) % count) for source in range(count)]
    return lax.ppermute(value, axis, pairs)


def layer_norm(rows):
    center = rows - jnp.mean(rows, -1, keepdims=True)
    spread = jnp.mean(center * center, -1, keepdims=True)
    return center * lax.rsqrt(spread + 1e-06)


def gelu_pair(pre):
    const = 0.7978845608028654
    inner = const * (pre + 0.044715 * pre * pre * pre)
    tanh_u = jnp.tanh(inner)
    value = 0.5 * pre * (1.0 + tanh_u)
    slope = 0.5 * (1.0 + tanh_u) + 0.5 * pre * (1.0 - tanh_u * tanh_u) * const * (
        1.0 + 3.0 * 0.044715 * pre * pre
    )
    return (value, slope)


def unit_rows(rows):
    scale = lax.rsqrt(jnp.sum(rows * rows, 1, keepdims=True) + 1e-06)
    return (rows * scale, scale)


def pair_coef(own_rows, own_group, other_rows, other_group):
    logits = (
        LOGIT_SCALE
        * lax.dot_general(
            own_rows, other_rows, (((1,), (1,)), ((), ())), preferred_element_type=jnp.float32
        )
        + LOGIT_SHIFT
    )
    signs = jnp.where(own_group[:, None] == other_group[None, :], 1.0, -1.0).astype(jnp.float32)
    coef = (-LOGIT_SCALE * signs * jax.nn.sigmoid(-signs * logits)).astype(jnp.bfloat16)
    return (logits, signs, coef)


def permuted_blocks(blocks, depth, first, second):
    lead = blocks.shape[:1]
    swap = dict(zip(first, second))
    split = blocks.reshape(lead + (2,) * depth + blocks.shape[2:])
    moved = [1 + depth - 1 - swap[depth - 1 - place] for place in range(depth)]
    axes = [0] + moved + list(range(1 + depth, split.ndim))
    return jnp.transpose(split, axes).reshape(blocks.shape)


def first_stage_halves(natural, permuted, variant):
    shape = natural.shape
    halves = shape[:1] + (shape[1] // 2, 2) + shape[2:]
    own = jnp.where(variant == 0, natural, permuted).reshape(halves)
    other = jnp.where(variant == 0, permuted, natural).reshape(halves)
    keep = lax.dynamic_index_in_dim(own, variant, axis=2, keepdims=False)
    send = lax.dynamic_index_in_dim(other, 1 - variant, axis=2, keepdims=False)
    return (keep, send)


def reduce_scatter_halving(keep, send, axis, first, second):
    devices = lax.axis_size(axis)
    own_index = lax.axis_index(axis)
    depth = devices.bit_length() - 1
    pairs = [(source, source ^ 1) for source in range(devices)]
    state = keep + lax.ppermute(send, axis, pairs)
    left = list(range(depth - 1, 0, -1))
    state = state.reshape((2,) * (depth - 1) + state.shape[1:])
    variant = own_index & 1
    for bit, twin in zip(first[1:], second[1:]):
        place = left.index(bit)
        own_bit = jnp.where(variant == 0, (own_index >> bit) & 1, (own_index >> twin) & 1)
        keep = lax.dynamic_index_in_dim(state, own_bit, axis=place, keepdims=False)
        send = lax.dynamic_index_in_dim(state, 1 - own_bit, axis=place, keepdims=False)
        pairs = [
            (source, source ^ (1 << (bit if source & 1 == 0 else twin)))
            for source in range(devices)
        ]
        state = keep + lax.ppermute(send, axis, pairs)
        left.remove(bit)
    return state


def all_gather_doubling(block, axis, order, companion=None, tie_at=0):
    devices = lax.axis_size(axis)
    own_index = lax.axis_index(axis)
    depth = devices.bit_length() - 1
    state = block[None]
    gathered = []
    for step, bit in enumerate(order):
        place = sum(1 for done in gathered if done > bit)
        pairs = [(source, source ^ (1 << bit)) for source in range(devices)]
        other = lax.ppermute(state, axis, pairs)
        if step == tie_at and companion is not None:
            other, companion = lax.optimization_barrier((other, companion))
        low_first = jnp.stack([state, other], axis=place)
        high_first = jnp.stack([other, state], axis=place)
        state = jnp.where(((own_index >> bit) & 1) == 0, low_first, high_first)
        gathered.append(bit)
    return (state.reshape((devices * block.shape[0],) + block.shape[1:]), companion)


def on_device(tokens, lengths, images, pair_group, w_up, w_down):
    captions = lengths.shape[0]
    seq_len = tokens.shape[0] // captions
    width = tokens.shape[1]
    hidden = w_up.shape[1]
    devices = lax.axis_size("dp")
    own_index = lax.axis_index("dp")
    total = captions * devices
    rows = width // devices
    own_group = lax.dynamic_slice_in_dim(pair_group, own_index * captions, captions)

    unit_image, image_scale = unit_rows(images.astype(jnp.float32))
    image_half = unit_image.astype(jnp.bfloat16)

    tok_float = tokens.astype(jnp.float32)
    normed = layer_norm(tok_float).astype(jnp.bfloat16)
    pre = jnp.dot(normed, w_up, preferred_element_type=jnp.float32)
    value, slope = gelu_pair(pre)
    position = jnp.arange(seq_len, dtype=jnp.int32)
    valid = (position[None, :] < lengths[:, None]).astype(jnp.float32)
    share = valid / jnp.sum(valid, 1, keepdims=True)
    owner = jnp.arange(captions * seq_len, dtype=jnp.int32) // seq_len
    share_rows = jnp.where(
        owner[None, :] == jnp.arange(captions, dtype=jnp.int32)[:, None],
        share.reshape(1, captions * seq_len),
        0.0,
    )
    gmean = jnp.dot(
        share_rows, value, precision=lax.Precision.HIGHEST, preferred_element_type=jnp.float32
    )
    tmean = jnp.sum(tok_float.reshape(captions, seq_len, width) * share[:, :, None], 1)
    gbar = gmean.astype(jnp.bfloat16)
    gbar_all, _ = all_gather_doubling(gbar, "dp", RS_TWIN[::-1])
    partial_value = lax.dot_general(
        gbar, w_down, (((1,), (1,)), ((), ())), preferred_element_type=jnp.float32
    )
    pooled = tmean + (partial_value + passed_along(partial_value, "mp", 1))
    unit_text, text_scale = unit_rows(pooled)
    text_half = unit_text.astype(jnp.bfloat16)
    normed_blocks = normed.reshape(captions * seq_len, devices, rows)
    depth = devices.bit_length() - 1
    keep_rows, send_rows = first_stage_halves(
        normed_blocks,
        permuted_blocks(normed_blocks, depth, RS_ORDER, RS_TWIN),
        own_index & 1,
    )
    both_all, (keep_rows, send_rows) = all_gather_doubling(
        jnp.concatenate([text_half, image_half], 1),
        "dp",
        RS_ORDER[::-1],
        (keep_rows, send_rows),
        len(RS_ORDER) - 2,
    )
    both_all, gbar_all = lax.optimization_barrier((both_all, gbar_all))
    text_all = both_all[:, :width]
    image_all = both_all[:, width:]

    logits, signs, coef = pair_coef(text_half, own_group, image_all, pair_group)
    caption_loss = -jnp.sum(jax.nn.log_sigmoid(signs * logits), 1) / total
    text_back = jnp.dot(coef, image_all, preferred_element_type=jnp.float32)
    _, _, coef_cols = pair_coef(image_half, own_group, text_all, pair_group)
    img_back = jnp.dot(coef_cols, text_all, preferred_element_type=jnp.float32)

    pooled_grad = (
        text_back - unit_text * jnp.sum(unit_text * text_back, 1, keepdims=True)
    ) * text_scale
    image_grad = (
        img_back - unit_image * jnp.sum(unit_image * img_back, 1, keepdims=True)
    ) * image_scale
    pooled_half = pooled_grad.astype(jnp.bfloat16)
    pooled_rows = lax.all_to_all(
        pooled_half.reshape(captions, devices, rows), "dp", 1, 0
    ).reshape(total, rows)
    down_grad = lax.dot_general(
        pooled_rows, gbar_all, (((0,), (0,)), ((), ())), preferred_element_type=jnp.float32
    )
    hidden_grad = jnp.dot(pooled_half, w_down, preferred_element_type=jnp.float32)
    spread_grad = lax.dot_general(
        share_rows,
        hidden_grad,
        (((0,), (0,)), ((), ())),
        precision=lax.Precision.HIGHEST,
        preferred_element_type=jnp.float32,
    )
    pre_grad = (spread_grad * slope).astype(jnp.bfloat16)
    keep_term, send_term = [
        lax.dot_general(
            part, pre_grad, (((0,), (0,)), ((), ())), preferred_element_type=jnp.float32
        )
        for part in (keep_rows, send_rows)
    ]
    up_grad = reduce_scatter_halving(keep_term, send_term, "dp", RS_ORDER, RS_TWIN)
    return (caption_loss, image_grad, up_grad, down_grad)


def solution(mesh):
    in_specs = (P("dp", None), P("dp"), P("dp", None), P(), P(None, "mp"), P(None, "mp"))
    out_specs = (P("dp"), P("dp", None), P("dp", "mp"), P("dp", "mp"))
    return jax.shard_map(
        on_device, mesh=mesh, in_specs=in_specs, out_specs=out_specs, check_vma=False
    )
```

```python
import jax
import jax.numpy as jnp
from jax import lax
from jax.sharding import PartitionSpec as P

LOGIT_SCALE = 117.0
LOGIT_SHIFT = -12.9
RS_ORDER = (0, 3, 1, 4, 2, 5)
RS_TWIN = (0, 4, 3, 1, 5, 2)


def passed_along(value, axis, steps):
    count = lax.axis_size(axis)
    pairs = [(source, (source + steps) % count) for source in range(count)]
    return lax.ppermute(value, axis, pairs)


def layer_norm(rows):
    center = rows - jnp.mean(rows, -1, keepdims=True)
    spread = jnp.mean(center * center, -1, keepdims=True)
    return center * lax.rsqrt(spread + 1e-06)


def gelu_pair(pre):
    const = 0.7978845608028654
    inner = const * (pre + 0.044715 * pre * pre * pre)
    tanh_u = jnp.tanh(inner)
    value = 0.5 * pre * (1.0 + tanh_u)
    slope = 0.5 * (1.0 + tanh_u) + 0.5 * pre * (1.0 - tanh_u * tanh_u) * const * (
        1.0 + 3.0 * 0.044715 * pre * pre
    )
    return (value, slope)


def unit_rows(rows):
    scale = lax.rsqrt(jnp.sum(rows * rows, 1, keepdims=True) + 1e-06)
    return (rows * scale, scale)


def pair_coef(own_rows, own_group, other_rows, other_group):
    logits = (
        LOGIT_SCALE
        * lax.dot_general(
            own_rows, other_rows, (((1,), (1,)), ((), ())), preferred_element_type=jnp.float32
        )
        + LOGIT_SHIFT
    )
    signs = jnp.where(own_group[:, None] == other_group[None, :], 1.0, -1.0).astype(jnp.float32)
    coef = (-LOGIT_SCALE * signs * jax.nn.sigmoid(-signs * logits)).astype(jnp.bfloat16)
    return (logits, signs, coef)


def permuted_blocks(blocks, depth, first, second):
    lead = blocks.shape[:1]
    swap = dict(zip(first, second))
    split = blocks.reshape(lead + (2,) * depth + blocks.shape[2:])
    moved = [1 + depth - 1 - swap[depth - 1 - place] for place in range(depth)]
    axes = [0] + moved + list(range(1 + depth, split.ndim))
    return jnp.transpose(split, axes).reshape(blocks.shape)


def first_stage_halves(natural, permuted, variant):
    shape = natural.shape
    halves = shape[:1] + (shape[1] // 2, 2) + shape[2:]
    own = jnp.where(variant == 0, natural, permuted).reshape(halves)
    other = jnp.where(variant == 0, permuted, natural).reshape(halves)
    keep = lax.dynamic_index_in_dim(own, variant, axis=2, keepdims=False)
    send = lax.dynamic_index_in_dim(other, 1 - variant, axis=2, keepdims=False)
    return (keep, send)


def reduce_scatter_halving(keep, send, axis, first, second):
    devices = lax.axis_size(axis)
    own_index = lax.axis_index(axis)
    depth = devices.bit_length() - 1
    pairs = [(source, source ^ 1) for source in range(devices)]
    state = keep + lax.ppermute(send, axis, pairs)
    left = list(range(depth - 1, 0, -1))
    state = state.reshape((2,) * (depth - 1) + state.shape[1:])
    variant = own_index & 1
    for bit, twin in zip(first[1:], second[1:]):
        place = left.index(bit)
        own_bit = jnp.where(variant == 0, (own_index >> bit) & 1, (own_index >> twin) & 1)
        keep = lax.dynamic_index_in_dim(state, own_bit, axis=place, keepdims=False)
        send = lax.dynamic_index_in_dim(state, 1 - own_bit, axis=place, keepdims=False)
        pairs = [
            (source, source ^ (1 << (bit if source & 1 == 0 else twin)))
            for source in range(devices)
        ]
        state = keep + lax.ppermute(send, axis, pairs)
        left.remove(bit)
    return state


def all_gather_doubling(block, axis, order, companion=None, tie_at=0):
    devices = lax.axis_size(axis)
    own_index = lax.axis_index(axis)
    depth = devices.bit_length() - 1
    state = block[None]
    gathered = []
    for step, bit in enumerate(order):
        place = sum(1 for done in gathered if done > bit)
        pairs = [(source, source ^ (1 << bit)) for source in range(devices)]
        other = lax.ppermute(state, axis, pairs)
        if step == tie_at and companion is not None:
            other, companion = lax.optimization_barrier((other, companion))
        low_first = jnp.stack([state, other], axis=place)
        high_first = jnp.stack([other, state], axis=place)
        state = jnp.where(((own_index >> bit) & 1) == 0, low_first, high_first)
        gathered.append(bit)
    return (state.reshape((devices * block.shape[0],) + block.shape[1:]), companion)


def on_device(tokens, lengths, images, pair_group, w_up, w_down):
    captions = lengths.shape[0]
    seq_len = tokens.shape[0] // captions
    width = tokens.shape[1]
    hidden = w_up.shape[1]
    devices = lax.axis_size("dp")
    own_index = lax.axis_index("dp")
    total = captions * devices
    rows = width // devices
    own_group = lax.dynamic_slice_in_dim(pair_group, own_index * captions, captions)

    unit_image, image_scale = unit_rows(images.astype(jnp.float32))
    image_half = unit_image.astype(jnp.bfloat16)

    tok_float = tokens.astype(jnp.float32)
    normed = layer_norm(tok_float).astype(jnp.bfloat16)
    pre = jnp.dot(normed, w_up, preferred_element_type=jnp.float32)
    value, slope = gelu_pair(pre)
    position = jnp.arange(seq_len, dtype=jnp.int32)
    valid = (position[None, :] < lengths[:, None]).astype(jnp.float32)
    share = valid / jnp.sum(valid, 1, keepdims=True)
    owner = jnp.arange(captions * seq_len, dtype=jnp.int32) // seq_len
    share_rows = jnp.where(
        owner[None, :] == jnp.arange(captions, dtype=jnp.int32)[:, None],
        share.reshape(1, captions * seq_len),
        0.0,
    )
    gmean = jnp.dot(
        share_rows, value, precision=lax.Precision.HIGHEST, preferred_element_type=jnp.float32
    )
    tmean = jnp.sum(tok_float.reshape(captions, seq_len, width) * share[:, :, None], 1)
    gbar = gmean.astype(jnp.bfloat16)
    gbar_all, _ = all_gather_doubling(gbar, "dp", RS_TWIN[::-1])
    partial_value = lax.dot_general(
        gbar, w_down, (((1,), (1,)), ((), ())), preferred_element_type=jnp.float32
    )
    pooled = tmean + (partial_value + passed_along(partial_value, "mp", 1))
    unit_text, text_scale = unit_rows(pooled)
    text_half = unit_text.astype(jnp.bfloat16)
    normed_late, pooled = lax.optimization_barrier((normed, pooled))
    normed_blocks = normed_late.reshape(captions * seq_len, devices, rows)
    depth = devices.bit_length() - 1
    keep_rows, send_rows = first_stage_halves(
        normed_blocks,
        permuted_blocks(normed_blocks, depth, RS_ORDER, RS_TWIN),
        own_index & 1,
    )
    both_all, (keep_rows, send_rows) = all_gather_doubling(
        jnp.concatenate([text_half, image_half], 1),
        "dp",
        RS_ORDER[::-1],
        (keep_rows, send_rows),
        len(RS_ORDER) - 2,
    )
    text_all = both_all[:, :width]
    image_all = both_all[:, width:]

    logits, signs, coef = pair_coef(text_half, own_group, image_all, pair_group)
    caption_loss = -jnp.sum(jax.nn.log_sigmoid(signs * logits), 1) / total
    text_back = jnp.dot(coef, image_all, preferred_element_type=jnp.float32)
    _, _, coef_cols = pair_coef(image_half, own_group, text_all, pair_group)
    img_back = jnp.dot(coef_cols, text_all, preferred_element_type=jnp.float32)

    pooled_grad = (
        text_back - unit_text * jnp.sum(unit_text * text_back, 1, keepdims=True)
    ) * text_scale
    image_grad = (
        img_back - unit_image * jnp.sum(unit_image * img_back, 1, keepdims=True)
    ) * image_scale
    pooled_half = pooled_grad.astype(jnp.bfloat16)
    pooled_half, gbar_all = lax.optimization_barrier((pooled_half, gbar_all))
    pooled_rows = lax.all_to_all(
        pooled_half.reshape(captions, devices, rows), "dp", 1, 0
    ).reshape(total, rows)
    down_grad = lax.dot_general(
        pooled_rows, gbar_all, (((0,), (0,)), ((), ())), preferred_element_type=jnp.float32
    )
    hidden_grad = jnp.dot(pooled_half, w_down, preferred_element_type=jnp.float32)
    spread_grad = lax.dot_general(
        share_rows,
        hidden_grad,
        (((0,), (0,)), ((), ())),
        precision=lax.Precision.HIGHEST,
        preferred_element_type=jnp.float32,
    )
    pre_grad = (spread_grad * slope).astype(jnp.bfloat16)
    keep_term, send_term = [
        lax.dot_general(
            part, pre_grad, (((0,), (0,)), ((), ())), preferred_element_type=jnp.float32
        )
        for part in (keep_rows, send_rows)
    ]
    up_grad = reduce_scatter_halving(keep_term, send_term, "dp", RS_ORDER, RS_TWIN)
    return (caption_loss, image_grad, up_grad, down_grad)


def solution(mesh):
    in_specs = (P("dp", None), P("dp"), P("dp", None), P(), P(None, "mp"), P(None, "mp"))
    out_specs = (P("dp"), P("dp", None), P("dp", "mp"), P("dp", "mp"))
    return jax.shard_map(
        on_device, mesh=mesh, in_specs=in_specs, out_specs=out_specs, check_vma=False
    )
```

```python
import jax
import jax.numpy as jnp
from jax import lax
from jax.sharding import PartitionSpec as P

LOGIT_SCALE = 117.0
LOGIT_SHIFT = -12.9
RS_ORDER = (0, 3, 1, 4, 2, 5)
RS_TWIN = (0, 4, 3, 1, 5, 2)


def passed_along(value, axis, steps):
    count = lax.axis_size(axis)
    pairs = [(source, (source + steps) % count) for source in range(count)]
    return lax.ppermute(value, axis, pairs)


def layer_norm(rows):
    center = rows - jnp.mean(rows, -1, keepdims=True)
    spread = jnp.mean(center * center, -1, keepdims=True)
    return center * lax.rsqrt(spread + 1e-06)


def gelu_pair(pre):
    const = 0.7978845608028654
    inner = const * (pre + 0.044715 * pre * pre * pre)
    tanh_u = jnp.tanh(inner)
    value = 0.5 * pre * (1.0 + tanh_u)
    slope = 0.5 * (1.0 + tanh_u) + 0.5 * pre * (1.0 - tanh_u * tanh_u) * const * (
        1.0 + 3.0 * 0.044715 * pre * pre
    )
    return (value, slope)


def unit_rows(rows):
    scale = lax.rsqrt(jnp.sum(rows * rows, 1, keepdims=True) + 1e-06)
    return (rows * scale, scale)


def pair_coef(own_rows, own_group, other_rows, other_group):
    logits = (
        LOGIT_SCALE
        * lax.dot_general(
            own_rows, other_rows, (((1,), (1,)), ((), ())), preferred_element_type=jnp.float32
        )
        + LOGIT_SHIFT
    )
    signs = jnp.where(own_group[:, None] == other_group[None, :], 1.0, -1.0).astype(jnp.float32)
    coef = (-LOGIT_SCALE * signs * jax.nn.sigmoid(-signs * logits)).astype(jnp.bfloat16)
    return (logits, signs, coef)


def permuted_blocks(blocks, depth, first, second):
    lead = blocks.shape[:1]
    swap = dict(zip(first, second))
    split = blocks.reshape(lead + (2,) * depth + blocks.shape[2:])
    moved = [1 + depth - 1 - swap[depth - 1 - place] for place in range(depth)]
    axes = [0] + moved + list(range(1 + depth, split.ndim))
    return jnp.transpose(split, axes).reshape(blocks.shape)


def first_stage_halves(natural, permuted, variant):
    shape = natural.shape
    halves = shape[:1] + (shape[1] // 2, 2) + shape[2:]
    own = jnp.where(variant == 0, natural, permuted).reshape(halves)
    other = jnp.where(variant == 0, permuted, natural).reshape(halves)
    keep = lax.dynamic_index_in_dim(own, variant, axis=2, keepdims=False)
    send = lax.dynamic_index_in_dim(other, 1 - variant, axis=2, keepdims=False)
    return (keep, send)


def reduce_scatter_halving(keep, send, axis, first, second, companion=None, tie_at=0):
    devices = lax.axis_size(axis)
    own_index = lax.axis_index(axis)
    depth = devices.bit_length() - 1
    pairs = [(source, source ^ 1) for source in range(devices)]
    state = keep + lax.ppermute(send, axis, pairs)
    left = list(range(depth - 1, 0, -1))
    state = state.reshape((2,) * (depth - 1) + state.shape[1:])
    variant = own_index & 1
    for step, (bit, twin) in enumerate(zip(first[1:], second[1:])):
        place = left.index(bit)
        own_bit = jnp.where(variant == 0, (own_index >> bit) & 1, (own_index >> twin) & 1)
        keep = lax.dynamic_index_in_dim(state, own_bit, axis=place, keepdims=False)
        send = lax.dynamic_index_in_dim(state, 1 - own_bit, axis=place, keepdims=False)
        pairs = [
            (source, source ^ (1 << (bit if source & 1 == 0 else twin)))
            for source in range(devices)
        ]
        received = lax.ppermute(send, axis, pairs)
        if step == tie_at and companion is not None:
            received, companion = lax.optimization_barrier((received, companion))
        state = keep + received
        left.remove(bit)
    return (state, companion)


def all_gather_doubling(block, axis, order, companion=None, tie_at=0):
    devices = lax.axis_size(axis)
    own_index = lax.axis_index(axis)
    depth = devices.bit_length() - 1
    state = block[None]
    gathered = []
    for step, bit in enumerate(order):
        place = sum(1 for done in gathered if done > bit)
        pairs = [(source, source ^ (1 << bit)) for source in range(devices)]
        other = lax.ppermute(state, axis, pairs)
        if step == tie_at and companion is not None:
            other, companion = lax.optimization_barrier((other, companion))
        low_first = jnp.stack([state, other], axis=place)
        high_first = jnp.stack([other, state], axis=place)
        state = jnp.where(((own_index >> bit) & 1) == 0, low_first, high_first)
        gathered.append(bit)
    return (state.reshape((devices * block.shape[0],) + block.shape[1:]), companion)


def on_device(tokens, lengths, images, pair_group, w_up, w_down):
    captions = lengths.shape[0]
    seq_len = tokens.shape[0] // captions
    width = tokens.shape[1]
    hidden = w_up.shape[1]
    devices = lax.axis_size("dp")
    own_index = lax.axis_index("dp")
    total = captions * devices
    rows = width // devices
    own_group = lax.dynamic_slice_in_dim(pair_group, own_index * captions, captions)

    unit_image, image_scale = unit_rows(images.astype(jnp.float32))
    image_half = unit_image.astype(jnp.bfloat16)

    tok_float = tokens.astype(jnp.float32)
    normed = layer_norm(tok_float).astype(jnp.bfloat16)
    pre = jnp.dot(normed, w_up, preferred_element_type=jnp.float32)
    value, slope = gelu_pair(pre)
    position = jnp.arange(seq_len, dtype=jnp.int32)
    valid = (position[None, :] < lengths[:, None]).astype(jnp.float32)
    share = valid / jnp.sum(valid, 1, keepdims=True)
    owner = jnp.arange(captions * seq_len, dtype=jnp.int32) // seq_len
    share_rows = jnp.where(
        owner[None, :] == jnp.arange(captions, dtype=jnp.int32)[:, None],
        share.reshape(1, captions * seq_len),
        0.0,
    )
    gmean = jnp.dot(
        share_rows, value, precision=lax.Precision.HIGHEST, preferred_element_type=jnp.float32
    )
    tmean = jnp.sum(tok_float.reshape(captions, seq_len, width) * share[:, :, None], 1)
    gbar = gmean.astype(jnp.bfloat16)
    gbar_all, _ = all_gather_doubling(gbar, "dp", RS_TWIN[::-1])
    partial_value = lax.dot_general(
        gbar, w_down, (((1,), (1,)), ((), ())), preferred_element_type=jnp.float32
    )
    pooled = tmean + (partial_value + passed_along(partial_value, "mp", 1))
    unit_text, text_scale = unit_rows(pooled)
    text_half = unit_text.astype(jnp.bfloat16)
    normed_late, pooled = lax.optimization_barrier((normed, pooled))
    normed_blocks = normed_late.reshape(captions * seq_len, devices, rows)
    depth = devices.bit_length() - 1
    keep_rows, send_rows = first_stage_halves(
        normed_blocks,
        permuted_blocks(normed_blocks, depth, RS_ORDER, RS_TWIN),
        own_index & 1,
    )
    both_all, (keep_rows, send_rows) = all_gather_doubling(
        jnp.concatenate([text_half, image_half], 1),
        "dp",
        RS_ORDER[::-1],
        (keep_rows, send_rows),
        len(RS_ORDER) - 2,
    )
    text_all = both_all[:, :width]
    image_all = both_all[:, width:]

    logits, signs, coef = pair_coef(text_half, own_group, image_all, pair_group)
    caption_loss = -jnp.sum(jax.nn.log_sigmoid(signs * logits), 1) / total
    text_back = jnp.dot(coef, image_all, preferred_element_type=jnp.float32)
    _, _, coef_cols = pair_coef(image_half, own_group, text_all, pair_group)
    img_back = jnp.dot(coef_cols, text_all, preferred_element_type=jnp.float32)

    pooled_grad = (
        text_back - unit_text * jnp.sum(unit_text * text_back, 1, keepdims=True)
    ) * text_scale
    image_grad = (
        img_back - unit_image * jnp.sum(unit_image * img_back, 1, keepdims=True)
    ) * image_scale
    pooled_half = pooled_grad.astype(jnp.bfloat16)
    pooled_half, gbar_all = lax.optimization_barrier((pooled_half, gbar_all))
    hidden_grad = jnp.dot(pooled_half, w_down, preferred_element_type=jnp.float32)
    spread_grad = lax.dot_general(
        share_rows,
        hidden_grad,
        (((0,), (0,)), ((), ())),
        precision=lax.Precision.HIGHEST,
        preferred_element_type=jnp.float32,
    )
    pre_grad = (spread_grad * slope).astype(jnp.bfloat16)
    keep_term, send_term = [
        lax.dot_general(
            part, pre_grad, (((0,), (0,)), ((), ())), preferred_element_type=jnp.float32
        )
        for part in (keep_rows, send_rows)
    ]
    pooled_rows = lax.all_to_all(
        pooled_half.reshape(captions, devices, rows), "dp", 1, 0
    ).reshape(total, rows)
    down_grad = lax.dot_general(
        pooled_rows, gbar_all, (((0,), (0,)), ((), ())), preferred_element_type=jnp.float32
    )
    up_grad, down_grad = reduce_scatter_halving(
        keep_term, send_term, "dp", RS_ORDER, RS_TWIN, down_grad, 0
    )
    return (caption_loss, image_grad, up_grad, down_grad)


def solution(mesh):
    in_specs = (P("dp", None), P("dp"), P("dp", None), P(), P(None, "mp"), P(None, "mp"))
    out_specs = (P("dp"), P("dp", None), P("dp", "mp"), P("dp", "mp"))
    return jax.shard_map(
        on_device, mesh=mesh, in_specs=in_specs, out_specs=out_specs, check_vma=False
    )
```

```python
import jax
import jax.numpy as jnp
from jax import lax
from jax.sharding import PartitionSpec as P

LOGIT_SCALE = 117.0
LOGIT_SHIFT = -12.9
RS_ORDER = (0, 3, 1, 4, 2, 5)
RS_TWIN = (0, 4, 3, 1, 5, 2)
RS_SECOND = ((0, 1, 4, 3, 5, 2), (0, 5, 2, 1, 3, 4))


def passed_along(value, axis, steps):
    count = lax.axis_size(axis)
    pairs = [(source, (source + steps) % count) for source in range(count)]
    return lax.ppermute(value, axis, pairs)


def layer_norm(rows):
    center = rows - jnp.mean(rows, -1, keepdims=True)
    spread = jnp.mean(center * center, -1, keepdims=True)
    return center * lax.rsqrt(spread + 1e-06)


def gelu_pair(pre):
    const = 0.7978845608028654
    inner = const * (pre + 0.044715 * pre * pre * pre)
    tanh_u = jnp.tanh(inner)
    value = 0.5 * pre * (1.0 + tanh_u)
    slope = 0.5 * (1.0 + tanh_u) + 0.5 * pre * (1.0 - tanh_u * tanh_u) * const * (
        1.0 + 3.0 * 0.044715 * pre * pre
    )
    return (value, slope)


def unit_rows(rows):
    scale = lax.rsqrt(jnp.sum(rows * rows, 1, keepdims=True) + 1e-06)
    return (rows * scale, scale)


def pair_coef(own_rows, own_group, other_rows, other_group):
    logits = (
        LOGIT_SCALE
        * lax.dot_general(
            own_rows, other_rows, (((1,), (1,)), ((), ())), preferred_element_type=jnp.float32
        )
        + LOGIT_SHIFT
    )
    signs = jnp.where(own_group[:, None] == other_group[None, :], 1.0, -1.0).astype(jnp.float32)
    coef = (-LOGIT_SCALE * signs * jax.nn.sigmoid(-signs * logits)).astype(jnp.bfloat16)
    return (logits, signs, coef)


def permuted_blocks(blocks, depth, first, second):
    lead = blocks.shape[:1]
    swap = dict(zip(first, second))
    split = blocks.reshape(lead + (2,) * depth + blocks.shape[2:])
    moved = [1 + depth - 1 - swap[depth - 1 - place] for place in range(depth)]
    axes = [0] + moved + list(range(1 + depth, split.ndim))
    return jnp.transpose(split, axes).reshape(blocks.shape)


def first_stage_halves(layout_even, layout_odd, variant):
    shape = layout_even.shape
    halves = shape[:1] + (shape[1] // 2, 2) + shape[2:]
    own = jnp.where(variant == 0, layout_even, layout_odd).reshape(halves)
    other = jnp.where(variant == 0, layout_odd, layout_even).reshape(halves)
    keep = lax.dynamic_index_in_dim(own, variant, axis=2, keepdims=False)
    send = lax.dynamic_index_in_dim(other, 1 - variant, axis=2, keepdims=False)
    return (keep, send)


def reduce_scatter_halving(keep, send, axis, labels, even, odd):
    devices = lax.axis_size(axis)
    own_index = lax.axis_index(axis)
    depth = devices.bit_length() - 1
    pairs = [(source, source ^ 1) for source in range(devices)]
    state = keep + lax.ppermute(send, axis, pairs)
    left = list(range(depth - 1, 0, -1))
    state = state.reshape((2,) * (depth - 1) + state.shape[1:])
    variant = own_index & 1
    for label, bit, twin in zip(labels[1:], even[1:], odd[1:]):
        place = left.index(label)
        own_bit = jnp.where(variant == 0, (own_index >> bit) & 1, (own_index >> twin) & 1)
        keep = lax.dynamic_index_in_dim(state, own_bit, axis=place, keepdims=False)
        send = lax.dynamic_index_in_dim(state, 1 - own_bit, axis=place, keepdims=False)
        pairs = [
            (source, source ^ (1 << (bit if source & 1 == 0 else twin)))
            for source in range(devices)
        ]
        state = keep + lax.ppermute(send, axis, pairs)
        left.remove(label)
    return state


def all_gather_doubling(block, axis, order, companion=None, tie_at=0):
    devices = lax.axis_size(axis)
    own_index = lax.axis_index(axis)
    depth = devices.bit_length() - 1
    state = block[None]
    gathered = []
    for step, bit in enumerate(order):
        place = sum(1 for done in gathered if done > bit)
        pairs = [(source, source ^ (1 << bit)) for source in range(devices)]
        other = lax.ppermute(state, axis, pairs)
        if step == tie_at and companion is not None:
            other, companion = lax.optimization_barrier((other, companion))
        low_first = jnp.stack([state, other], axis=place)
        high_first = jnp.stack([other, state], axis=place)
        state = jnp.where(((own_index >> bit) & 1) == 0, low_first, high_first)
        gathered.append(bit)
    return (state.reshape((devices * block.shape[0],) + block.shape[1:]), companion)


def on_device(tokens, lengths, images, pair_group, w_up, w_down):
    captions = lengths.shape[0]
    seq_len = tokens.shape[0] // captions
    width = tokens.shape[1]
    hidden = w_up.shape[1]
    devices = lax.axis_size("dp")
    own_index = lax.axis_index("dp")
    total = captions * devices
    rows = width // devices
    own_group = lax.dynamic_slice_in_dim(pair_group, own_index * captions, captions)

    unit_image, image_scale = unit_rows(images.astype(jnp.float32))
    image_half = unit_image.astype(jnp.bfloat16)

    tok_float = tokens.astype(jnp.float32)
    normed = layer_norm(tok_float).astype(jnp.bfloat16)
    pre = jnp.dot(normed, w_up, preferred_element_type=jnp.float32)
    value, slope = gelu_pair(pre)
    position = jnp.arange(seq_len, dtype=jnp.int32)
    valid = (position[None, :] < lengths[:, None]).astype(jnp.float32)
    share = valid / jnp.sum(valid, 1, keepdims=True)
    owner = jnp.arange(captions * seq_len, dtype=jnp.int32) // seq_len
    share_rows = jnp.where(
        owner[None, :] == jnp.arange(captions, dtype=jnp.int32)[:, None],
        share.reshape(1, captions * seq_len),
        0.0,
    )
    gmean = jnp.dot(
        share_rows, value, precision=lax.Precision.HIGHEST, preferred_element_type=jnp.float32
    )
    tmean = jnp.sum(tok_float.reshape(captions, seq_len, width) * share[:, :, None], 1)
    gbar = gmean.astype(jnp.bfloat16)
    gbar_all, _ = all_gather_doubling(gbar, "dp", RS_TWIN[::-1])
    partial_value = lax.dot_general(
        gbar, w_down, (((1,), (1,)), ((), ())), preferred_element_type=jnp.float32
    )
    pooled = tmean + (partial_value + passed_along(partial_value, "mp", 1))
    unit_text, text_scale = unit_rows(pooled)
    text_half = unit_text.astype(jnp.bfloat16)
    normed_late, pooled = lax.optimization_barrier((normed, pooled))
    normed_blocks = normed_late.reshape(captions * seq_len, devices, rows)
    depth = devices.bit_length() - 1
    chunk_orders = ((RS_ORDER, RS_TWIN), RS_SECOND)
    row_halves = tuple(
        first_stage_halves(
            permuted_blocks(normed_blocks, depth, RS_ORDER, even),
            permuted_blocks(normed_blocks, depth, RS_ORDER, odd),
            own_index & 1,
        )
        for even, odd in chunk_orders
    )
    both_all, row_halves = all_gather_doubling(
        jnp.concatenate([text_half, image_half], 1),
        "dp",
        RS_ORDER[::-1],
        row_halves,
        len(RS_ORDER) - 2,
    )
    text_all = both_all[:, :width]
    image_all = both_all[:, width:]

    logits, signs, coef = pair_coef(text_half, own_group, image_all, pair_group)
    caption_loss = -jnp.sum(jax.nn.log_sigmoid(signs * logits), 1) / total
    text_back = jnp.dot(coef, image_all, preferred_element_type=jnp.float32)
    _, _, coef_cols = pair_coef(image_half, own_group, text_all, pair_group)
    img_back = jnp.dot(coef_cols, text_all, preferred_element_type=jnp.float32)

    pooled_grad = (
        text_back - unit_text * jnp.sum(unit_text * text_back, 1, keepdims=True)
    ) * text_scale
    image_grad = (
        img_back - unit_image * jnp.sum(unit_image * img_back, 1, keepdims=True)
    ) * image_scale
    pooled_half = pooled_grad.astype(jnp.bfloat16)
    pooled_half, gbar_all = lax.optimization_barrier((pooled_half, gbar_all))
    pooled_rows = lax.all_to_all(
        pooled_half.reshape(captions, devices, rows), "dp", 1, 0
    ).reshape(total, rows)
    down_grad = lax.dot_general(
        pooled_rows, gbar_all, (((0,), (0,)), ((), ())), preferred_element_type=jnp.float32
    )
    hidden_grad = jnp.dot(pooled_half, w_down, preferred_element_type=jnp.float32)
    spread_grad = lax.dot_general(
        share_rows,
        hidden_grad,
        (((0,), (0,)), ((), ())),
        precision=lax.Precision.HIGHEST,
        preferred_element_type=jnp.float32,
    )
    pre_grad = (spread_grad * slope).astype(jnp.bfloat16)
    half = hidden // 2
    grad_chunks = (pre_grad[:, :half], pre_grad[:, half:])
    pieces = []
    for (keep_rows, send_rows), (even, odd), grad_chunk in zip(
        row_halves, chunk_orders, grad_chunks
    ):
        keep_term, send_term = [
            lax.dot_general(
                part, grad_chunk, (((0,), (0,)), ((), ())), preferred_element_type=jnp.float32
            )
            for part in (keep_rows, send_rows)
        ]
        pieces.append(reduce_scatter_halving(keep_term, send_term, "dp", RS_ORDER, even, odd))
    up_grad = jnp.concatenate(pieces, 1)
    return (caption_loss, image_grad, up_grad, down_grad)


def solution(mesh):
    in_specs = (P("dp", None), P("dp"), P("dp", None), P(), P(None, "mp"), P(None, "mp"))
    out_specs = (P("dp"), P("dp", None), P("dp", "mp"), P("dp", "mp"))
    return jax.shard_map(
        on_device, mesh=mesh, in_specs=in_specs, out_specs=out_specs, check_vma=False
    )
```

```python
import jax
import jax.numpy as jnp
from jax import lax
from jax.sharding import PartitionSpec as P

LOGIT_SCALE = 117.0
LOGIT_SHIFT = -12.9
RS_ORDER = (0, 3, 1, 4, 2, 5)
RS_TWIN = (0, 4, 3, 1, 5, 2)


def passed_along(value, axis, steps):
    count = lax.axis_size(axis)
    pairs = [(source, (source + steps) % count) for source in range(count)]
    return lax.ppermute(value, axis, pairs)


def layer_norm(rows):
    center = rows - jnp.mean(rows, -1, keepdims=True)
    spread = jnp.mean(center * center, -1, keepdims=True)
    return center * lax.rsqrt(spread + 1e-06)


def gelu_pair(pre):
    const = 0.7978845608028654
    inner = const * (pre + 0.044715 * pre * pre * pre)
    tanh_u = jnp.tanh(inner)
    value = 0.5 * pre * (1.0 + tanh_u)
    slope = 0.5 * (1.0 + tanh_u) + 0.5 * pre * (1.0 - tanh_u * tanh_u) * const * (
        1.0 + 3.0 * 0.044715 * pre * pre
    )
    return (value, slope)


def unit_rows(rows):
    scale = lax.rsqrt(jnp.sum(rows * rows, 1, keepdims=True) + 1e-06)
    return (rows * scale, scale)


def pair_coef(own_rows, own_group, other_rows, other_group):
    logits = (
        LOGIT_SCALE
        * lax.dot_general(
            own_rows, other_rows, (((1,), (1,)), ((), ())), preferred_element_type=jnp.float32
        )
        + LOGIT_SHIFT
    )
    signs = jnp.where(own_group[:, None] == other_group[None, :], 1.0, -1.0).astype(jnp.float32)
    coef = (-LOGIT_SCALE * signs * jax.nn.sigmoid(-signs * logits)).astype(jnp.bfloat16)
    return (logits, signs, coef)


def permuted_blocks(blocks, depth, first, second):
    lead = blocks.shape[:1]
    swap = dict(zip(first, second))
    split = blocks.reshape(lead + (2,) * depth + blocks.shape[2:])
    moved = [1 + depth - 1 - swap[depth - 1 - place] for place in range(depth)]
    axes = [0] + moved + list(range(1 + depth, split.ndim))
    return jnp.transpose(split, axes).reshape(blocks.shape)


def first_stage_halves(natural, permuted, variant):
    shape = natural.shape
    halves = shape[:1] + (shape[1] // 2, 2) + shape[2:]
    own = jnp.where(variant == 0, natural, permuted).reshape(halves)
    other = jnp.where(variant == 0, permuted, natural).reshape(halves)
    keep = lax.dynamic_index_in_dim(own, variant, axis=2, keepdims=False)
    send = lax.dynamic_index_in_dim(other, 1 - variant, axis=2, keepdims=False)
    return (keep, send)


def reduce_scatter_halving(keep, send, axis, first, second):
    devices = lax.axis_size(axis)
    own_index = lax.axis_index(axis)
    depth = devices.bit_length() - 1
    pairs = [(source, source ^ 1) for source in range(devices)]
    state = keep + lax.ppermute(send, axis, pairs)
    left = list(range(depth - 1, 0, -1))
    state = state.reshape((2,) * (depth - 1) + state.shape[1:])
    variant = own_index & 1
    for bit, twin in zip(first[1:], second[1:]):
        place = left.index(bit)
        own_bit = jnp.where(variant == 0, (own_index >> bit) & 1, (own_index >> twin) & 1)
        keep = lax.dynamic_index_in_dim(state, own_bit, axis=place, keepdims=False)
        send = lax.dynamic_index_in_dim(state, 1 - own_bit, axis=place, keepdims=False)
        pairs = [
            (source, source ^ (1 << (bit if source & 1 == 0 else twin)))
            for source in range(devices)
        ]
        state = keep + lax.ppermute(send, axis, pairs)
        left.remove(bit)
    return state


def all_gather_doubling(block, axis, order, companion=None, tie_at=0):
    devices = lax.axis_size(axis)
    own_index = lax.axis_index(axis)
    depth = devices.bit_length() - 1
    state = block[None]
    gathered = []
    for step, bit in enumerate(order):
        place = sum(1 for done in gathered if done > bit)
        pairs = [(source, source ^ (1 << bit)) for source in range(devices)]
        other = lax.ppermute(state, axis, pairs)
        if step == tie_at and companion is not None:
            other, companion = lax.optimization_barrier((other, companion))
        low_first = jnp.stack([state, other], axis=place)
        high_first = jnp.stack([other, state], axis=place)
        state = jnp.where(((own_index >> bit) & 1) == 0, low_first, high_first)
        gathered.append(bit)
    return (state.reshape((devices * block.shape[0],) + block.shape[1:]), companion)


def on_device(tokens, lengths, images, pair_group, w_up, w_down):
    captions = lengths.shape[0]
    seq_len = tokens.shape[0] // captions
    width = tokens.shape[1]
    hidden = w_up.shape[1]
    devices = lax.axis_size("dp")
    own_index = lax.axis_index("dp")
    total = captions * devices
    rows = width // devices
    own_group = lax.dynamic_slice_in_dim(pair_group, own_index * captions, captions)

    unit_image, image_scale = unit_rows(images.astype(jnp.float32))
    image_half = unit_image.astype(jnp.bfloat16)

    tok_float = tokens.astype(jnp.float32)
    normed = layer_norm(tok_float).astype(jnp.bfloat16)
    pre = jnp.dot(normed, w_up, preferred_element_type=jnp.float32)
    value, slope = gelu_pair(pre)
    position = jnp.arange(seq_len, dtype=jnp.int32)
    valid = (position[None, :] < lengths[:, None]).astype(jnp.float32)
    share = valid / jnp.sum(valid, 1, keepdims=True)
    owner = jnp.arange(captions * seq_len, dtype=jnp.int32) // seq_len
    share_rows = jnp.where(
        owner[None, :] == jnp.arange(captions, dtype=jnp.int32)[:, None],
        share.reshape(1, captions * seq_len),
        0.0,
    )
    gmean = jnp.dot(
        share_rows, value, precision=lax.Precision.HIGHEST, preferred_element_type=jnp.float32
    )
    tmean = jnp.sum(tok_float.reshape(captions, seq_len, width) * share[:, :, None], 1)
    gbar = gmean.astype(jnp.bfloat16)
    gbar_all, _ = all_gather_doubling(gbar, "dp", RS_TWIN[::-1])
    partial_value = lax.dot_general(
        gbar, w_down, (((1,), (1,)), ((), ())), preferred_element_type=jnp.float32
    )
    pooled = tmean + (partial_value + passed_along(partial_value, "mp", 1))
    unit_text, text_scale = unit_rows(pooled)
    text_half = unit_text.astype(jnp.bfloat16)
    normed_late, pooled = lax.optimization_barrier((normed, pooled))
    normed_blocks = normed_late.reshape(captions * seq_len, devices, rows)
    depth = devices.bit_length() - 1
    keep_rows, send_rows = first_stage_halves(
        normed_blocks,
        permuted_blocks(normed_blocks, depth, RS_ORDER, RS_TWIN),
        own_index & 1,
    )
    both_all, (keep_rows, send_rows) = all_gather_doubling(
        jnp.concatenate([text_half, image_half], 1),
        "dp",
        RS_ORDER[::-1],
        (keep_rows, send_rows),
        len(RS_ORDER) - 1,
    )
    text_all = both_all[:, :width]
    image_all = both_all[:, width:]

    logits, signs, coef = pair_coef(text_half, own_group, image_all, pair_group)
    caption_loss = -jnp.sum(jax.nn.log_sigmoid(signs * logits), 1) / total
    text_back = jnp.dot(coef, image_all, preferred_element_type=jnp.float32)
    _, _, coef_cols = pair_coef(image_half, own_group, text_all, pair_group)
    img_back = jnp.dot(coef_cols, text_all, preferred_element_type=jnp.float32)

    pooled_grad = (
        text_back - unit_text * jnp.sum(unit_text * text_back, 1, keepdims=True)
    ) * text_scale
    image_grad = (
        img_back - unit_image * jnp.sum(unit_image * img_back, 1, keepdims=True)
    ) * image_scale
    pooled_half = pooled_grad.astype(jnp.bfloat16)
    pooled_half, gbar_all = lax.optimization_barrier((pooled_half, gbar_all))
    pooled_rows = lax.all_to_all(
        pooled_half.reshape(captions, devices, rows), "dp", 1, 0
    ).reshape(total, rows)
    down_grad = lax.dot_general(
        pooled_rows, gbar_all, (((0,), (0,)), ((), ())), preferred_element_type=jnp.float32
    )
    hidden_grad = jnp.dot(pooled_half, w_down, preferred_element_type=jnp.float32)
    spread_grad = lax.dot_general(
        share_rows,
        hidden_grad,
        (((0,), (0,)), ((), ())),
        precision=lax.Precision.HIGHEST,
        preferred_element_type=jnp.float32,
    )
    pre_grad = (spread_grad * slope).astype(jnp.bfloat16)
    keep_term, send_term = [
        lax.dot_general(
            part, pre_grad, (((0,), (0,)), ((), ())), preferred_element_type=jnp.float32
        )
        for part in (keep_rows, send_rows)
    ]
    up_grad = reduce_scatter_halving(keep_term, send_term, "dp", RS_ORDER, RS_TWIN)
    return (caption_loss, image_grad, up_grad, down_grad)


def solution(mesh):
    in_specs = (P("dp", None), P("dp"), P("dp", None), P(), P(None, "mp"), P(None, "mp"))
    out_specs = (P("dp"), P("dp", None), P("dp", "mp"), P("dp", "mp"))
    return jax.shard_map(
        on_device, mesh=mesh, in_specs=in_specs, out_specs=out_specs, check_vma=False
    )
```

```python
import jax
import jax.numpy as jnp
from jax import lax
from jax.sharding import PartitionSpec as P

LOGIT_SCALE = 117.0
LOGIT_SHIFT = -12.9
RS_ORDER = (0, 3, 1, 4, 2, 5)
RS_TWIN = (0, 4, 3, 1, 5, 2)
RS_LABELS = (0, 5, 4, 3, 2, 1)


def passed_along(value, axis, steps):
    count = lax.axis_size(axis)
    pairs = [(source, (source + steps) % count) for source in range(count)]
    return lax.ppermute(value, axis, pairs)


def layer_norm(rows):
    center = rows - jnp.mean(rows, -1, keepdims=True)
    spread = jnp.mean(center * center, -1, keepdims=True)
    return center * lax.rsqrt(spread + 1e-06)


def gelu_pair(pre):
    const = 0.7978845608028654
    inner = const * (pre + 0.044715 * pre * pre * pre)
    tanh_u = jnp.tanh(inner)
    value = 0.5 * pre * (1.0 + tanh_u)
    slope = 0.5 * (1.0 + tanh_u) + 0.5 * pre * (1.0 - tanh_u * tanh_u) * const * (
        1.0 + 3.0 * 0.044715 * pre * pre
    )
    return (value, slope)


def unit_rows(rows):
    scale = lax.rsqrt(jnp.sum(rows * rows, 1, keepdims=True) + 1e-06)
    return (rows * scale, scale)


def pair_coef(own_rows, own_group, other_rows, other_group):
    logits = (
        LOGIT_SCALE
        * lax.dot_general(
            own_rows, other_rows, (((1,), (1,)), ((), ())), preferred_element_type=jnp.float32
        )
        + LOGIT_SHIFT
    )
    signs = jnp.where(own_group[:, None] == other_group[None, :], 1.0, -1.0).astype(jnp.float32)
    coef = (-LOGIT_SCALE * signs * jax.nn.sigmoid(-signs * logits)).astype(jnp.bfloat16)
    return (logits, signs, coef)


def permuted_blocks(blocks, depth, first, second):
    lead = blocks.shape[:1]
    swap = dict(zip(first, second))
    split = blocks.reshape(lead + (2,) * depth + blocks.shape[2:])
    moved = [1 + depth - 1 - swap[depth - 1 - place] for place in range(depth)]
    axes = [0] + moved + list(range(1 + depth, split.ndim))
    return jnp.transpose(split, axes).reshape(blocks.shape)


def first_stage_halves(natural, permuted, variant):
    shape = natural.shape
    halves = shape[:1] + (shape[1] // 2, 2) + shape[2:]
    own = jnp.where(variant == 0, natural, permuted).reshape(halves)
    other = jnp.where(variant == 0, permuted, natural).reshape(halves)
    keep = lax.dynamic_index_in_dim(own, variant, axis=2, keepdims=False)
    send = lax.dynamic_index_in_dim(other, 1 - variant, axis=2, keepdims=False)
    return (keep, send)


def reduce_scatter_halving(keep, send, axis, first, second):
    devices = lax.axis_size(axis)
    own_index = lax.axis_index(axis)
    pairs = [(source, source ^ 1) for source in range(devices)]
    state = keep + lax.ppermute(send, axis, pairs)
    variant = own_index & 1
    for bit, twin in zip(first[1:], second[1:]):
        size = state.shape[0] // 2
        own_bit = jnp.where(variant == 0, (own_index >> bit) & 1, (own_index >> twin) & 1)
        keep = lax.dynamic_slice_in_dim(state, own_bit * size, size, axis=0)
        send = lax.dynamic_slice_in_dim(state, (1 - own_bit) * size, size, axis=0)
        pairs = [
            (source, source ^ (1 << (bit if source & 1 == 0 else twin)))
            for source in range(devices)
        ]
        state = keep + lax.ppermute(send, axis, pairs)
    return state[0]


def all_gather_doubling(block, axis, order, companion=None, tie_at=0):
    devices = lax.axis_size(axis)
    own_index = lax.axis_index(axis)
    depth = devices.bit_length() - 1
    state = block[None]
    gathered = []
    for step, bit in enumerate(order):
        place = sum(1 for done in gathered if done > bit)
        pairs = [(source, source ^ (1 << bit)) for source in range(devices)]
        other = lax.ppermute(state, axis, pairs)
        if step == tie_at and companion is not None:
            other, companion = lax.optimization_barrier((other, companion))
        low_first = jnp.stack([state, other], axis=place)
        high_first = jnp.stack([other, state], axis=place)
        state = jnp.where(((own_index >> bit) & 1) == 0, low_first, high_first)
        gathered.append(bit)
    return (state.reshape((devices * block.shape[0],) + block.shape[1:]), companion)


def on_device(tokens, lengths, images, pair_group, w_up, w_down):
    captions = lengths.shape[0]
    seq_len = tokens.shape[0] // captions
    width = tokens.shape[1]
    hidden = w_up.shape[1]
    devices = lax.axis_size("dp")
    own_index = lax.axis_index("dp")
    total = captions * devices
    rows = width // devices
    own_group = lax.dynamic_slice_in_dim(pair_group, own_index * captions, captions)

    unit_image, image_scale = unit_rows(images.astype(jnp.float32))
    image_half = unit_image.astype(jnp.bfloat16)

    tok_float = tokens.astype(jnp.float32)
    normed = layer_norm(tok_float).astype(jnp.bfloat16)
    pre = jnp.dot(normed, w_up, preferred_element_type=jnp.float32)
    value, slope = gelu_pair(pre)
    position = jnp.arange(seq_len, dtype=jnp.int32)
    valid = (position[None, :] < lengths[:, None]).astype(jnp.float32)
    share = valid / jnp.sum(valid, 1, keepdims=True)
    owner = jnp.arange(captions * seq_len, dtype=jnp.int32) // seq_len
    share_rows = jnp.where(
        owner[None, :] == jnp.arange(captions, dtype=jnp.int32)[:, None],
        share.reshape(1, captions * seq_len),
        0.0,
    )
    gmean = jnp.dot(
        share_rows, value, precision=lax.Precision.HIGHEST, preferred_element_type=jnp.float32
    )
    tmean = jnp.sum(tok_float.reshape(captions, seq_len, width) * share[:, :, None], 1)
    gbar = gmean.astype(jnp.bfloat16)
    gbar_all, _ = all_gather_doubling(gbar, "dp", RS_TWIN[::-1])
    partial_value = lax.dot_general(
        gbar, w_down, (((1,), (1,)), ((), ())), preferred_element_type=jnp.float32
    )
    pooled = tmean + (partial_value + passed_along(partial_value, "mp", 1))
    unit_text, text_scale = unit_rows(pooled)
    text_half = unit_text.astype(jnp.bfloat16)
    normed_late, pooled = lax.optimization_barrier((normed, pooled))
    normed_blocks = normed_late.reshape(captions * seq_len, devices, rows)
    depth = devices.bit_length() - 1
    keep_rows, send_rows = first_stage_halves(
        permuted_blocks(normed_blocks, depth, RS_LABELS, RS_ORDER),
        permuted_blocks(normed_blocks, depth, RS_LABELS, RS_TWIN),
        own_index & 1,
    )
    both_all, (keep_rows, send_rows) = all_gather_doubling(
        jnp.concatenate([text_half, image_half], 1),
        "dp",
        RS_ORDER[::-1],
        (keep_rows, send_rows),
        len(RS_ORDER) - 2,
    )
    text_all = both_all[:, :width]
    image_all = both_all[:, width:]

    logits, signs, coef = pair_coef(text_half, own_group, image_all, pair_group)
    caption_loss = -jnp.sum(jax.nn.log_sigmoid(signs * logits), 1) / total
    text_back = jnp.dot(coef, image_all, preferred_element_type=jnp.float32)
    _, _, coef_cols = pair_coef(image_half, own_group, text_all, pair_group)
    img_back = jnp.dot(coef_cols, text_all, preferred_element_type=jnp.float32)

    pooled_grad = (
        text_back - unit_text * jnp.sum(unit_text * text_back, 1, keepdims=True)
    ) * text_scale
    image_grad = (
        img_back - unit_image * jnp.sum(unit_image * img_back, 1, keepdims=True)
    ) * image_scale
    pooled_half = pooled_grad.astype(jnp.bfloat16)
    pooled_half, gbar_all = lax.optimization_barrier((pooled_half, gbar_all))
    pooled_rows = lax.all_to_all(
        pooled_half.reshape(captions, devices, rows), "dp", 1, 0
    ).reshape(total, rows)
    down_grad = lax.dot_general(
        pooled_rows, gbar_all, (((0,), (0,)), ((), ())), preferred_element_type=jnp.float32
    )
    hidden_grad = jnp.dot(pooled_half, w_down, preferred_element_type=jnp.float32)
    spread_grad = lax.dot_general(
        share_rows,
        hidden_grad,
        (((0,), (0,)), ((), ())),
        precision=lax.Precision.HIGHEST,
        preferred_element_type=jnp.float32,
    )
    pre_grad = (spread_grad * slope).astype(jnp.bfloat16)
    keep_term, send_term = [
        lax.dot_general(
            part, pre_grad, (((0,), (0,)), ((), ())), preferred_element_type=jnp.float32
        )
        for part in (keep_rows, send_rows)
    ]
    up_grad = reduce_scatter_halving(keep_term, send_term, "dp", RS_ORDER, RS_TWIN)
    return (caption_loss, image_grad, up_grad, down_grad)


def solution(mesh):
    in_specs = (P("dp", None), P("dp"), P("dp", None), P(), P(None, "mp"), P(None, "mp"))
    out_specs = (P("dp"), P("dp", None), P("dp", "mp"), P("dp", "mp"))
    return jax.shard_map(
        on_device, mesh=mesh, in_specs=in_specs, out_specs=out_specs, check_vma=False
    )
```

```python
import jax
import jax.numpy as jnp
from jax import lax
from jax.sharding import PartitionSpec as P

LOGIT_SCALE = 117.0
LOGIT_SHIFT = -12.9
RS_ORDER = (0, 3, 1, 4, 2, 5)
RS_TWIN = (0, 4, 3, 1, 5, 2)
RS_LABELS = (0, 5, 4, 3, 2, 1)


def passed_along(value, axis, steps):
    count = lax.axis_size(axis)
    pairs = [(source, (source + steps) % count) for source in range(count)]
    return lax.ppermute(value, axis, pairs)


def layer_norm(rows):
    center = rows - jnp.mean(rows, -1, keepdims=True)
    spread = jnp.mean(center * center, -1, keepdims=True)
    return center * lax.rsqrt(spread + 1e-06)


def gelu_pair(pre):
    const = 0.7978845608028654
    inner = const * (pre + 0.044715 * pre * pre * pre)
    tanh_u = jnp.tanh(inner)
    value = 0.5 * pre * (1.0 + tanh_u)
    slope = 0.5 * (1.0 + tanh_u) + 0.5 * pre * (1.0 - tanh_u * tanh_u) * const * (
        1.0 + 3.0 * 0.044715 * pre * pre
    )
    return (value, slope)


def unit_rows(rows):
    scale = lax.rsqrt(jnp.sum(rows * rows, 1, keepdims=True) + 1e-06)
    return (rows * scale, scale)


def pair_coef(own_rows, own_group, other_rows, other_group):
    logits = (
        LOGIT_SCALE
        * lax.dot_general(
            own_rows, other_rows, (((1,), (1,)), ((), ())), preferred_element_type=jnp.float32
        )
        + LOGIT_SHIFT
    )
    signs = jnp.where(own_group[:, None] == other_group[None, :], 1.0, -1.0).astype(jnp.float32)
    coef = (-LOGIT_SCALE * signs * jax.nn.sigmoid(-signs * logits)).astype(jnp.bfloat16)
    return (logits, signs, coef)


def permuted_blocks(blocks, depth, first, second):
    lead = blocks.shape[:1]
    swap = dict(zip(first, second))
    split = blocks.reshape(lead + (2,) * depth + blocks.shape[2:])
    moved = [1 + depth - 1 - swap[depth - 1 - place] for place in range(depth)]
    axes = [0] + moved + list(range(1 + depth, split.ndim))
    return jnp.transpose(split, axes).reshape(blocks.shape)


def first_stage_halves(natural, permuted, variant):
    shape = natural.shape
    halves = shape[:1] + (shape[1] // 2, 2) + shape[2:]
    own = jnp.where(variant == 0, natural, permuted).reshape(halves)
    other = jnp.where(variant == 0, permuted, natural).reshape(halves)
    keep = lax.dynamic_index_in_dim(own, variant, axis=2, keepdims=False)
    send = lax.dynamic_index_in_dim(other, 1 - variant, axis=2, keepdims=False)
    return (keep, send)


def reduce_scatter_halving(keep, send, axis, first, second):
    devices = lax.axis_size(axis)
    own_index = lax.axis_index(axis)
    pairs = [(source, source ^ 1) for source in range(devices)]
    state = keep + lax.ppermute(send, axis, pairs)
    variant = own_index & 1
    for bit, twin in zip(first[1:], second[1:]):
        size = state.shape[0] // 2
        own_bit = jnp.where(variant == 0, (own_index >> bit) & 1, (own_index >> twin) & 1)
        keep = lax.dynamic_slice_in_dim(state, own_bit * size, size, axis=0)
        send = lax.dynamic_slice_in_dim(state, (1 - own_bit) * size, size, axis=0)
        pairs = [
            (source, source ^ (1 << (bit if source & 1 == 0 else twin)))
            for source in range(devices)
        ]
        state = keep + lax.ppermute(send, axis, pairs)
    return state[0]


def all_gather_doubling(block, axis, order, companion=None, tie_at=0):
    devices = lax.axis_size(axis)
    own_index = lax.axis_index(axis)
    depth = devices.bit_length() - 1
    state = block[None]
    gathered = []
    for step, bit in enumerate(order):
        place = sum(1 for done in gathered if done > bit)
        pairs = [(source, source ^ (1 << bit)) for source in range(devices)]
        other = lax.ppermute(state, axis, pairs)
        if step == tie_at and companion is not None:
            other, companion = lax.optimization_barrier((other, companion))
        low_first = jnp.stack([state, other], axis=place)
        high_first = jnp.stack([other, state], axis=place)
        state = jnp.where(((own_index >> bit) & 1) == 0, low_first, high_first)
        gathered.append(bit)
    return (state.reshape((devices * block.shape[0],) + block.shape[1:]), companion)


def all_gather_appending(block, axis, order, companion=None, tie_at=0):
    devices = lax.axis_size(axis)
    own_index = lax.axis_index(axis)
    state = block
    for step, bit in enumerate(order):
        pairs = [(source, source ^ (1 << bit)) for source in range(devices)]
        other = lax.ppermute(state, axis, pairs)
        if step == tie_at and companion is not None:
            other, companion = lax.optimization_barrier((other, companion))
        state = jnp.concatenate([state, other], 0)
    table = [sum(((spot >> step) & 1) << bit for step, bit in enumerate(order)) for spot in range(devices)]
    sources = jnp.bitwise_xor(jnp.asarray(table, jnp.int32), own_index)
    return (state, sources, companion)


def on_device(tokens, lengths, images, pair_group, w_up, w_down):
    captions = lengths.shape[0]
    seq_len = tokens.shape[0] // captions
    width = tokens.shape[1]
    hidden = w_up.shape[1]
    devices = lax.axis_size("dp")
    own_index = lax.axis_index("dp")
    total = captions * devices
    rows = width // devices
    own_group = lax.dynamic_slice_in_dim(pair_group, own_index * captions, captions)

    unit_image, image_scale = unit_rows(images.astype(jnp.float32))
    image_half = unit_image.astype(jnp.bfloat16)

    tok_float = tokens.astype(jnp.float32)
    normed = layer_norm(tok_float).astype(jnp.bfloat16)
    pre = jnp.dot(normed, w_up, preferred_element_type=jnp.float32)
    value, slope = gelu_pair(pre)
    position = jnp.arange(seq_len, dtype=jnp.int32)
    valid = (position[None, :] < lengths[:, None]).astype(jnp.float32)
    share = valid / jnp.sum(valid, 1, keepdims=True)
    owner = jnp.arange(captions * seq_len, dtype=jnp.int32) // seq_len
    share_rows = jnp.where(
        owner[None, :] == jnp.arange(captions, dtype=jnp.int32)[:, None],
        share.reshape(1, captions * seq_len),
        0.0,
    )
    gmean = jnp.dot(
        share_rows, value, precision=lax.Precision.HIGHEST, preferred_element_type=jnp.float32
    )
    tmean = jnp.sum(tok_float.reshape(captions, seq_len, width) * share[:, :, None], 1)
    gbar = gmean.astype(jnp.bfloat16)
    gbar_all, _ = all_gather_doubling(gbar, "dp", RS_TWIN[::-1])
    partial_value = lax.dot_general(
        gbar, w_down, (((1,), (1,)), ((), ())), preferred_element_type=jnp.float32
    )
    pooled = tmean + (partial_value + passed_along(partial_value, "mp", 1))
    unit_text, text_scale = unit_rows(pooled)
    text_half = unit_text.astype(jnp.bfloat16)
    normed_late, pooled = lax.optimization_barrier((normed, pooled))
    normed_blocks = normed_late.reshape(captions * seq_len, devices, rows)
    depth = devices.bit_length() - 1
    keep_rows, send_rows = first_stage_halves(
        permuted_blocks(normed_blocks, depth, RS_LABELS, RS_ORDER),
        permuted_blocks(normed_blocks, depth, RS_LABELS, RS_TWIN),
        own_index & 1,
    )
    both_all, sources, (keep_rows, send_rows) = all_gather_appending(
        jnp.concatenate([text_half, image_half], 1),
        "dp",
        RS_ORDER[::-1],
        (keep_rows, send_rows),
        len(RS_ORDER) - 2,
    )
    text_all = both_all[:, :width]
    image_all = both_all[:, width:]
    slot = sources[:, None] * captions + jnp.arange(captions, dtype=jnp.int32)[None, :]
    arrived_group = jnp.take(pair_group, slot.reshape(total), axis=0)

    logits, signs, coef = pair_coef(text_half, own_group, image_all, arrived_group)
    caption_loss = -jnp.sum(jax.nn.log_sigmoid(signs * logits), 1) / total
    text_back = jnp.dot(coef, image_all, preferred_element_type=jnp.float32)
    _, _, coef_cols = pair_coef(image_half, own_group, text_all, arrived_group)
    img_back = jnp.dot(coef_cols, text_all, preferred_element_type=jnp.float32)

    pooled_grad = (
        text_back - unit_text * jnp.sum(unit_text * text_back, 1, keepdims=True)
    ) * text_scale
    image_grad = (
        img_back - unit_image * jnp.sum(unit_image * img_back, 1, keepdims=True)
    ) * image_scale
    pooled_half = pooled_grad.astype(jnp.bfloat16)
    pooled_half, gbar_all = lax.optimization_barrier((pooled_half, gbar_all))
    pooled_rows = lax.all_to_all(
        pooled_half.reshape(captions, devices, rows), "dp", 1, 0
    ).reshape(total, rows)
    down_grad = lax.dot_general(
        pooled_rows, gbar_all, (((0,), (0,)), ((), ())), preferred_element_type=jnp.float32
    )
    hidden_grad = jnp.dot(pooled_half, w_down, preferred_element_type=jnp.float32)
    spread_grad = lax.dot_general(
        share_rows,
        hidden_grad,
        (((0,), (0,)), ((), ())),
        precision=lax.Precision.HIGHEST,
        preferred_element_type=jnp.float32,
    )
    pre_grad = (spread_grad * slope).astype(jnp.bfloat16)
    keep_term, send_term = [
        lax.dot_general(
            part, pre_grad, (((0,), (0,)), ((), ())), preferred_element_type=jnp.float32
        )
        for part in (keep_rows, send_rows)
    ]
    up_grad = reduce_scatter_halving(keep_term, send_term, "dp", RS_ORDER, RS_TWIN)
    return (caption_loss, image_grad, up_grad, down_grad)


def solution(mesh):
    in_specs = (P("dp", None), P("dp"), P("dp", None), P(), P(None, "mp"), P(None, "mp"))
    out_specs = (P("dp"), P("dp", None), P("dp", "mp"), P("dp", "mp"))
    return jax.shard_map(
        on_device, mesh=mesh, in_specs=in_specs, out_specs=out_specs, check_vma=False
    )
```

```python
import jax
import jax.numpy as jnp
from jax import lax
from jax.sharding import PartitionSpec as P

LOGIT_SCALE = 117.0
LOGIT_SHIFT = -12.9
RS_ORDER = (0, 3, 1, 4, 2, 5)
RS_TWIN = (0, 4, 3, 1, 5, 2)
RS_LABELS = (0, 5, 4, 3, 2, 1)


def passed_along(value, axis, steps):
    count = lax.axis_size(axis)
    pairs = [(source, (source + steps) % count) for source in range(count)]
    return lax.ppermute(value, axis, pairs)


def layer_norm(rows):
    center = rows - jnp.mean(rows, -1, keepdims=True)
    spread = jnp.mean(center * center, -1, keepdims=True)
    return center * lax.rsqrt(spread + 1e-06)


def gelu_pair(pre):
    const = 0.7978845608028654
    inner = const * (pre + 0.044715 * pre * pre * pre)
    tanh_u = jnp.tanh(inner)
    value = 0.5 * pre * (1.0 + tanh_u)
    slope = 0.5 * (1.0 + tanh_u) + 0.5 * pre * (1.0 - tanh_u * tanh_u) * const * (
        1.0 + 3.0 * 0.044715 * pre * pre
    )
    return (value, slope)


def unit_rows(rows):
    scale = lax.rsqrt(jnp.sum(rows * rows, 1, keepdims=True) + 1e-06)
    return (rows * scale, scale)


def pair_coef(own_rows, own_group, other_rows, other_group):
    logits = (
        LOGIT_SCALE
        * lax.dot_general(
            own_rows, other_rows, (((1,), (1,)), ((), ())), preferred_element_type=jnp.float32
        )
        + LOGIT_SHIFT
    )
    signs = jnp.where(own_group[:, None] == other_group[None, :], 1.0, -1.0).astype(jnp.float32)
    coef = (-LOGIT_SCALE * signs * jax.nn.sigmoid(-signs * logits)).astype(jnp.bfloat16)
    return (logits, signs, coef)


def permuted_blocks(blocks, depth, first, second):
    lead = blocks.shape[:1]
    swap = dict(zip(first, second))
    split = blocks.reshape(lead + (2,) * depth + blocks.shape[2:])
    moved = [1 + depth - 1 - swap[depth - 1 - place] for place in range(depth)]
    axes = [0] + moved + list(range(1 + depth, split.ndim))
    return jnp.transpose(split, axes).reshape(blocks.shape)


def first_stage_halves(natural, permuted, variant):
    shape = natural.shape
    halves = shape[:1] + (shape[1] // 2, 2) + shape[2:]
    own = jnp.where(variant == 0, natural, permuted).reshape(halves)
    other = jnp.where(variant == 0, permuted, natural).reshape(halves)
    keep = lax.dynamic_index_in_dim(own, variant, axis=2, keepdims=False)
    send = lax.dynamic_index_in_dim(other, 1 - variant, axis=2, keepdims=False)
    return (keep, send)


def reduce_scatter_halving(keep, send, axis, first, second):
    devices = lax.axis_size(axis)
    own_index = lax.axis_index(axis)
    pairs = [(source, source ^ 1) for source in range(devices)]
    state = keep + lax.ppermute(send, axis, pairs)
    variant = own_index & 1
    for bit, twin in zip(first[1:], second[1:]):
        size = state.shape[0] // 2
        own_bit = jnp.where(variant == 0, (own_index >> bit) & 1, (own_index >> twin) & 1)
        keep = lax.dynamic_slice_in_dim(state, own_bit * size, size, axis=0)
        send = lax.dynamic_slice_in_dim(state, (1 - own_bit) * size, size, axis=0)
        pairs = [
            (source, source ^ (1 << (bit if source & 1 == 0 else twin)))
            for source in range(devices)
        ]
        state = keep + lax.ppermute(send, axis, pairs)
    return state[0]


def all_gather_doubling(block, axis, order, companion=None, tie_at=0):
    devices = lax.axis_size(axis)
    own_index = lax.axis_index(axis)
    depth = devices.bit_length() - 1
    state = block[None]
    gathered = []
    for step, bit in enumerate(order):
        place = sum(1 for done in gathered if done > bit)
        pairs = [(source, source ^ (1 << bit)) for source in range(devices)]
        other = lax.ppermute(state, axis, pairs)
        if step == tie_at and companion is not None:
            other, companion = lax.optimization_barrier((other, companion))
        low_first = jnp.stack([state, other], axis=place)
        high_first = jnp.stack([other, state], axis=place)
        state = jnp.where(((own_index >> bit) & 1) == 0, low_first, high_first)
        gathered.append(bit)
    return (state.reshape((devices * block.shape[0],) + block.shape[1:]), companion)


def on_device(tokens, lengths, images, pair_group, w_up, w_down):
    captions = lengths.shape[0]
    seq_len = tokens.shape[0] // captions
    width = tokens.shape[1]
    hidden = w_up.shape[1]
    devices = lax.axis_size("dp")
    own_index = lax.axis_index("dp")
    total = captions * devices
    rows = width // devices
    own_group = lax.dynamic_slice_in_dim(pair_group, own_index * captions, captions)

    unit_image, image_scale = unit_rows(images.astype(jnp.float32))
    image_half = unit_image.astype(jnp.bfloat16)

    tok_float = tokens.astype(jnp.float32)
    normed = layer_norm(tok_float).astype(jnp.bfloat16)
    pre = jnp.dot(normed, w_up, preferred_element_type=jnp.float32)
    value, slope = gelu_pair(pre)
    position = jnp.arange(seq_len, dtype=jnp.int32)
    valid = (position[None, :] < lengths[:, None]).astype(jnp.float32)
    share = valid / jnp.sum(valid, 1, keepdims=True)
    owner = jnp.arange(captions * seq_len, dtype=jnp.int32) // seq_len
    share_rows = jnp.where(
        owner[None, :] == jnp.arange(captions, dtype=jnp.int32)[:, None],
        share.reshape(1, captions * seq_len),
        0.0,
    )
    gmean = jnp.dot(
        share_rows, value, precision=lax.Precision.HIGHEST, preferred_element_type=jnp.float32
    )
    tmean = jnp.sum(tok_float.reshape(captions, seq_len, width) * share[:, :, None], 1)
    gbar = gmean.astype(jnp.bfloat16)
    gbar_all, _ = all_gather_doubling(gbar, "dp", RS_TWIN[::-1])
    partial_value = lax.dot_general(
        gbar, w_down, (((1,), (1,)), ((), ())), preferred_element_type=jnp.float32
    )
    pooled = tmean + (partial_value + passed_along(partial_value, "mp", 1))
    unit_text, text_scale = unit_rows(pooled)
    text_half = unit_text.astype(jnp.bfloat16)
    normed_late, pooled = lax.optimization_barrier((normed, pooled))
    normed_blocks = normed_late.reshape(captions * seq_len, devices, rows)
    depth = devices.bit_length() - 1
    keep_rows, send_rows = first_stage_halves(
        permuted_blocks(normed_blocks, depth, RS_LABELS, RS_ORDER),
        permuted_blocks(normed_blocks, depth, RS_LABELS, RS_TWIN),
        own_index & 1,
    )
    both_all, (keep_rows, send_rows) = all_gather_doubling(
        jnp.concatenate([text_half, image_half], 1),
        "dp",
        RS_ORDER[::-1],
        (keep_rows, send_rows),
        len(RS_ORDER) - 2,
    )
    text_all = both_all[:, :width]
    image_all = both_all[:, width:]

    logits, signs, coef = pair_coef(text_half, own_group, image_all, pair_group)
    caption_loss = -jnp.sum(jax.nn.log_sigmoid(signs * logits), 1) / total
    text_back = jnp.dot(coef, image_all, preferred_element_type=jnp.float32)
    _, _, coef_cols = pair_coef(image_half, own_group, text_all, pair_group)
    img_back = jnp.dot(coef_cols, text_all, preferred_element_type=jnp.float32)

    pooled_grad = (
        text_back - unit_text * jnp.sum(unit_text * text_back, 1, keepdims=True)
    ) * text_scale
    image_grad = (
        img_back - unit_image * jnp.sum(unit_image * img_back, 1, keepdims=True)
    ) * image_scale
    pooled_half = pooled_grad.astype(jnp.bfloat16)
    pooled_half, gbar_all = lax.optimization_barrier((pooled_half, gbar_all))
    pooled_rows = lax.all_to_all(
        pooled_half.reshape(captions, devices, rows), "dp", 1, 0
    ).reshape(total, rows)
    down_grad = lax.dot_general(
        pooled_rows, gbar_all, (((0,), (0,)), ((), ())), preferred_element_type=jnp.float32
    )
    hidden_grad = jnp.dot(pooled_half, w_down, preferred_element_type=jnp.float32)
    spread_grad = lax.dot_general(
        share_rows,
        hidden_grad,
        (((0,), (0,)), ((), ())),
        precision=lax.Precision.HIGHEST,
        preferred_element_type=jnp.float32,
    )
    pre_grad = (spread_grad * slope).astype(jnp.bfloat16)
    keep_term, send_term = [
        lax.dot_general(
            part, pre_grad, (((0,), (0,)), ((), ())), preferred_element_type=jnp.float32
        )
        for part in (keep_rows, send_rows)
    ]
    keep_term = lax.optimization_barrier(keep_term)
    up_grad = reduce_scatter_halving(keep_term, send_term, "dp", RS_ORDER, RS_TWIN)
    return (caption_loss, image_grad, up_grad, down_grad)


def solution(mesh):
    in_specs = (P("dp", None), P("dp"), P("dp", None), P(), P(None, "mp"), P(None, "mp"))
    out_specs = (P("dp"), P("dp", None), P("dp", "mp"), P("dp", "mp"))
    return jax.shard_map(
        on_device, mesh=mesh, in_specs=in_specs, out_specs=out_specs, check_vma=False
    )
```

```python
import jax
import jax.numpy as jnp
from jax import lax
from jax.sharding import PartitionSpec as P

LOGIT_SCALE = 117.0
LOGIT_SHIFT = -12.9
RS_ORDER = (0, 3, 1, 4, 2, 5)
RS_TWIN = (0, 4, 3, 1, 5, 2)
RS_LABELS = (0, 5, 4, 3, 2, 1)


def passed_along(value, axis, steps):
    count = lax.axis_size(axis)
    pairs = [(source, (source + steps) % count) for source in range(count)]
    return lax.ppermute(value, axis, pairs)


def layer_norm(rows):
    center = rows - jnp.mean(rows, -1, keepdims=True)
    spread = jnp.mean(center * center, -1, keepdims=True)
    return center * lax.rsqrt(spread + 1e-06)


def gelu_pair(pre):
    const = 0.7978845608028654
    inner = const * (pre + 0.044715 * pre * pre * pre)
    tanh_u = jnp.tanh(inner)
    value = 0.5 * pre * (1.0 + tanh_u)
    slope = 0.5 * (1.0 + tanh_u) + 0.5 * pre * (1.0 - tanh_u * tanh_u) * const * (
        1.0 + 3.0 * 0.044715 * pre * pre
    )
    return (value, slope)


def unit_rows(rows):
    scale = lax.rsqrt(jnp.sum(rows * rows, 1, keepdims=True) + 1e-06)
    return (rows * scale, scale)


def pair_coef(own_rows, own_group, other_rows, other_group):
    logits = (
        LOGIT_SCALE
        * lax.dot_general(
            own_rows, other_rows, (((1,), (1,)), ((), ())), preferred_element_type=jnp.float32
        )
        + LOGIT_SHIFT
    )
    signs = jnp.where(own_group[:, None] == other_group[None, :], 1.0, -1.0).astype(jnp.float32)
    coef = (-LOGIT_SCALE * signs * jax.nn.sigmoid(-signs * logits)).astype(jnp.bfloat16)
    return (logits, signs, coef)


def permuted_blocks(blocks, depth, first, second):
    lead = blocks.shape[:1]
    swap = dict(zip(first, second))
    split = blocks.reshape(lead + (2,) * depth + blocks.shape[2:])
    moved = [1 + depth - 1 - swap[depth - 1 - place] for place in range(depth)]
    axes = [0] + moved + list(range(1 + depth, split.ndim))
    return jnp.transpose(split, axes).reshape(blocks.shape)


def first_stage_halves(natural, permuted, variant):
    shape = natural.shape
    halves = shape[:1] + (shape[1] // 2, 2) + shape[2:]
    own = jnp.where(variant == 0, natural, permuted).reshape(halves)
    other = jnp.where(variant == 0, permuted, natural).reshape(halves)
    keep = lax.dynamic_index_in_dim(own, variant, axis=2, keepdims=False)
    send = lax.dynamic_index_in_dim(other, 1 - variant, axis=2, keepdims=False)
    return (keep, send)


def reduce_scatter_halving(keep, send, axis, first, second, companion=None, tie_at=0):
    devices = lax.axis_size(axis)
    own_index = lax.axis_index(axis)
    pairs = [(source, source ^ 1) for source in range(devices)]
    state = keep + lax.ppermute(send, axis, pairs)
    variant = own_index & 1
    for step, (bit, twin) in enumerate(zip(first[1:], second[1:])):
        size = state.shape[0] // 2
        own_bit = jnp.where(variant == 0, (own_index >> bit) & 1, (own_index >> twin) & 1)
        keep = lax.dynamic_slice_in_dim(state, own_bit * size, size, axis=0)
        send = lax.dynamic_slice_in_dim(state, (1 - own_bit) * size, size, axis=0)
        pairs = [
            (source, source ^ (1 << (bit if source & 1 == 0 else twin)))
            for source in range(devices)
        ]
        received = lax.ppermute(send, axis, pairs)
        if step == tie_at and companion is not None:
            received, companion = lax.optimization_barrier((received, companion))
        state = keep + received
    return (state[0], companion)


def all_gather_doubling(block, axis, order, companion=None, tie_at=0):
    devices = lax.axis_size(axis)
    own_index = lax.axis_index(axis)
    depth = devices.bit_length() - 1
    state = block[None]
    gathered = []
    for step, bit in enumerate(order):
        place = sum(1 for done in gathered if done > bit)
        pairs = [(source, source ^ (1 << bit)) for source in range(devices)]
        other = lax.ppermute(state, axis, pairs)
        if step == tie_at and companion is not None:
            other, companion = lax.optimization_barrier((other, companion))
        low_first = jnp.stack([state, other], axis=place)
        high_first = jnp.stack([other, state], axis=place)
        state = jnp.where(((own_index >> bit) & 1) == 0, low_first, high_first)
        gathered.append(bit)
    return (state.reshape((devices * block.shape[0],) + block.shape[1:]), companion)


def on_device(tokens, lengths, images, pair_group, w_up, w_down):
    captions = lengths.shape[0]
    seq_len = tokens.shape[0] // captions
    width = tokens.shape[1]
    hidden = w_up.shape[1]
    devices = lax.axis_size("dp")
    own_index = lax.axis_index("dp")
    total = captions * devices
    rows = width // devices
    own_group = lax.dynamic_slice_in_dim(pair_group, own_index * captions, captions)

    unit_image, image_scale = unit_rows(images.astype(jnp.float32))
    image_half = unit_image.astype(jnp.bfloat16)

    tok_float = tokens.astype(jnp.float32)
    normed = layer_norm(tok_float).astype(jnp.bfloat16)
    pre = jnp.dot(normed, w_up, preferred_element_type=jnp.float32)
    value, slope = gelu_pair(pre)
    position = jnp.arange(seq_len, dtype=jnp.int32)
    valid = (position[None, :] < lengths[:, None]).astype(jnp.float32)
    share = valid / jnp.sum(valid, 1, keepdims=True)
    owner = jnp.arange(captions * seq_len, dtype=jnp.int32) // seq_len
    share_rows = jnp.where(
        owner[None, :] == jnp.arange(captions, dtype=jnp.int32)[:, None],
        share.reshape(1, captions * seq_len),
        0.0,
    )
    gmean = jnp.dot(
        share_rows, value, precision=lax.Precision.HIGHEST, preferred_element_type=jnp.float32
    )
    tmean = jnp.sum(tok_float.reshape(captions, seq_len, width) * share[:, :, None], 1)
    gbar = gmean.astype(jnp.bfloat16)
    gbar_all, _ = all_gather_doubling(gbar, "dp", RS_TWIN[::-1])
    partial_value = lax.dot_general(
        gbar, w_down, (((1,), (1,)), ((), ())), preferred_element_type=jnp.float32
    )
    pooled = tmean + (partial_value + passed_along(partial_value, "mp", 1))
    unit_text, text_scale = unit_rows(pooled)
    text_half = unit_text.astype(jnp.bfloat16)
    normed_late, pooled = lax.optimization_barrier((normed, pooled))
    normed_blocks = normed_late.reshape(captions * seq_len, devices, rows)
    depth = devices.bit_length() - 1
    keep_rows, send_rows = first_stage_halves(
        permuted_blocks(normed_blocks, depth, RS_LABELS, RS_ORDER),
        permuted_blocks(normed_blocks, depth, RS_LABELS, RS_TWIN),
        own_index & 1,
    )
    both_all, (keep_rows, send_rows) = all_gather_doubling(
        jnp.concatenate([text_half, image_half], 1),
        "dp",
        RS_ORDER[::-1],
        (keep_rows, send_rows),
        len(RS_ORDER) - 2,
    )
    text_all = both_all[:, :width]
    image_all = both_all[:, width:]

    logits, signs, coef = pair_coef(text_half, own_group, image_all, pair_group)
    caption_loss = -jnp.sum(jax.nn.log_sigmoid(signs * logits), 1) / total
    text_back = jnp.dot(coef, image_all, preferred_element_type=jnp.float32)
    _, _, coef_cols = pair_coef(image_half, own_group, text_all, pair_group)
    img_back = jnp.dot(coef_cols, text_all, preferred_element_type=jnp.float32)

    pooled_grad = (
        text_back - unit_text * jnp.sum(unit_text * text_back, 1, keepdims=True)
    ) * text_scale
    image_grad = (
        img_back - unit_image * jnp.sum(unit_image * img_back, 1, keepdims=True)
    ) * image_scale
    pooled_half = pooled_grad.astype(jnp.bfloat16)
    pooled_half, gbar_all = lax.optimization_barrier((pooled_half, gbar_all))
    hidden_grad = jnp.dot(pooled_half, w_down, preferred_element_type=jnp.float32)
    spread_grad = lax.dot_general(
        share_rows,
        hidden_grad,
        (((0,), (0,)), ((), ())),
        precision=lax.Precision.HIGHEST,
        preferred_element_type=jnp.float32,
    )
    pre_grad = (spread_grad * slope).astype(jnp.bfloat16)
    keep_term, send_term = [
        lax.dot_general(
            part, pre_grad, (((0,), (0,)), ((), ())), preferred_element_type=jnp.float32
        )
        for part in (keep_rows, send_rows)
    ]
    keep_term = lax.optimization_barrier(keep_term)
    pooled_rows = lax.all_to_all(
        pooled_half.reshape(captions, devices, rows), "dp", 1, 0
    ).reshape(total, rows)
    down_grad = lax.dot_general(
        pooled_rows, gbar_all, (((0,), (0,)), ((), ())), preferred_element_type=jnp.float32
    )
    up_grad, down_grad = reduce_scatter_halving(
        keep_term, send_term, "dp", RS_ORDER, RS_TWIN, down_grad, 2
    )
    return (caption_loss, image_grad, up_grad, down_grad)


def solution(mesh):
    in_specs = (P("dp", None), P("dp"), P("dp", None), P(), P(None, "mp"), P(None, "mp"))
    out_specs = (P("dp"), P("dp", None), P("dp", "mp"), P("dp", "mp"))
    return jax.shard_map(
        on_device, mesh=mesh, in_specs=in_specs, out_specs=out_specs, check_vma=False
    )
```

```python
import jax
import jax.numpy as jnp
from jax import lax
from jax.sharding import PartitionSpec as P

LOGIT_SCALE = 117.0
LOGIT_SHIFT = -12.9
RS_ORDER = (0, 3, 1, 4, 2, 5)
RS_TWIN = (0, 4, 3, 1, 5, 2)
RS_LABELS = (0, 5, 4, 3, 2, 1)


def passed_along(value, axis, steps):
    count = lax.axis_size(axis)
    pairs = [(source, (source + steps) % count) for source in range(count)]
    return lax.ppermute(value, axis, pairs)


def layer_norm(rows):
    center = rows - jnp.mean(rows, -1, keepdims=True)
    spread = jnp.mean(center * center, -1, keepdims=True)
    return center * lax.rsqrt(spread + 1e-06)


def gelu_pair(pre):
    const = 0.7978845608028654
    inner = const * (pre + 0.044715 * pre * pre * pre)
    tanh_u = jnp.tanh(inner)
    value = 0.5 * pre * (1.0 + tanh_u)
    slope = 0.5 * (1.0 + tanh_u) + 0.5 * pre * (1.0 - tanh_u * tanh_u) * const * (
        1.0 + 3.0 * 0.044715 * pre * pre
    )
    return (value, slope)


def unit_rows(rows):
    scale = lax.rsqrt(jnp.sum(rows * rows, 1, keepdims=True) + 1e-06)
    return (rows * scale, scale)


def pair_coef(own_rows, own_group, other_rows, other_group):
    logits = (
        LOGIT_SCALE
        * lax.dot_general(
            own_rows, other_rows, (((1,), (1,)), ((), ())), preferred_element_type=jnp.float32
        )
        + LOGIT_SHIFT
    )
    signs = jnp.where(own_group[:, None] == other_group[None, :], 1.0, -1.0).astype(jnp.float32)
    coef = (-LOGIT_SCALE * signs * jax.nn.sigmoid(-signs * logits)).astype(jnp.bfloat16)
    return (logits, signs, coef)


def permuted_blocks(blocks, depth, first, second):
    lead = blocks.shape[:1]
    swap = dict(zip(first, second))
    split = blocks.reshape(lead + (2,) * depth + blocks.shape[2:])
    moved = [1 + depth - 1 - swap[depth - 1 - place] for place in range(depth)]
    axes = [0] + moved + list(range(1 + depth, split.ndim))
    return jnp.transpose(split, axes).reshape(blocks.shape)


def first_stage_halves(natural, permuted, variant):
    shape = natural.shape
    halves = shape[:1] + (shape[1] // 2, 2) + shape[2:]
    own = jnp.where(variant == 0, natural, permuted).reshape(halves)
    other = jnp.where(variant == 0, permuted, natural).reshape(halves)
    keep = lax.dynamic_index_in_dim(own, variant, axis=2, keepdims=False)
    send = lax.dynamic_index_in_dim(other, 1 - variant, axis=2, keepdims=False)
    return (keep, send)


def reduce_scatter_halving(keep, send, axis, first, second, companion=None, tie_at=0):
    devices = lax.axis_size(axis)
    own_index = lax.axis_index(axis)
    pairs = [(source, source ^ 1) for source in range(devices)]
    state = keep + lax.ppermute(send, axis, pairs)
    variant = own_index & 1
    for step, (bit, twin) in enumerate(zip(first[1:], second[1:])):
        size = state.shape[0] // 2
        own_bit = jnp.where(variant == 0, (own_index >> bit) & 1, (own_index >> twin) & 1)
        keep = lax.dynamic_slice_in_dim(state, own_bit * size, size, axis=0)
        send = lax.dynamic_slice_in_dim(state, (1 - own_bit) * size, size, axis=0)
        pairs = [
            (source, source ^ (1 << (bit if source & 1 == 0 else twin)))
            for source in range(devices)
        ]
        received = lax.ppermute(send, axis, pairs)
        if step == tie_at and companion is not None:
            received, companion = lax.optimization_barrier((received, companion))
        state = keep + received
    return (state[0], companion)


def all_gather_doubling(block, axis, order, companion=None, tie_at=0):
    devices = lax.axis_size(axis)
    own_index = lax.axis_index(axis)
    depth = devices.bit_length() - 1
    state = block[None]
    gathered = []
    for step, bit in enumerate(order):
        place = sum(1 for done in gathered if done > bit)
        pairs = [(source, source ^ (1 << bit)) for source in range(devices)]
        other = lax.ppermute(state, axis, pairs)
        if step == tie_at and companion is not None:
            other, companion = lax.optimization_barrier((other, companion))
        low_first = jnp.stack([state, other], axis=place)
        high_first = jnp.stack([other, state], axis=place)
        state = jnp.where(((own_index >> bit) & 1) == 0, low_first, high_first)
        gathered.append(bit)
    return (state.reshape((devices * block.shape[0],) + block.shape[1:]), companion)


def on_device(tokens, lengths, images, pair_group, w_up, w_down):
    captions = lengths.shape[0]
    seq_len = tokens.shape[0] // captions
    width = tokens.shape[1]
    hidden = w_up.shape[1]
    devices = lax.axis_size("dp")
    own_index = lax.axis_index("dp")
    total = captions * devices
    rows = width // devices
    own_group = lax.dynamic_slice_in_dim(pair_group, own_index * captions, captions)

    unit_image, image_scale = unit_rows(images.astype(jnp.float32))
    image_half = unit_image.astype(jnp.bfloat16)

    tok_float = tokens.astype(jnp.float32)
    normed = layer_norm(tok_float).astype(jnp.bfloat16)
    pre = jnp.dot(normed, w_up, preferred_element_type=jnp.float32)
    value, slope = gelu_pair(pre)
    position = jnp.arange(seq_len, dtype=jnp.int32)
    valid = (position[None, :] < lengths[:, None]).astype(jnp.float32)
    share = valid / jnp.sum(valid, 1, keepdims=True)
    owner = jnp.arange(captions * seq_len, dtype=jnp.int32) // seq_len
    share_rows = jnp.where(
        owner[None, :] == jnp.arange(captions, dtype=jnp.int32)[:, None],
        share.reshape(1, captions * seq_len),
        0.0,
    )
    gmean = jnp.dot(
        share_rows, value, precision=lax.Precision.HIGHEST, preferred_element_type=jnp.float32
    )
    tmean = jnp.sum(tok_float.reshape(captions, seq_len, width) * share[:, :, None], 1)
    gbar = gmean.astype(jnp.bfloat16)
    gbar_all, _ = all_gather_doubling(gbar, "dp", RS_TWIN[::-1])
    partial_value = lax.dot_general(
        gbar, w_down, (((1,), (1,)), ((), ())), preferred_element_type=jnp.float32
    )
    pooled = tmean + (partial_value + passed_along(partial_value, "mp", 1))
    unit_text, text_scale = unit_rows(pooled)
    text_half = unit_text.astype(jnp.bfloat16)
    normed_late, pooled = lax.optimization_barrier((normed, pooled))
    normed_blocks = normed_late.reshape(captions * seq_len, devices, rows)
    depth = devices.bit_length() - 1
    keep_rows, send_rows = first_stage_halves(
        permuted_blocks(normed_blocks, depth, RS_LABELS, RS_ORDER),
        permuted_blocks(normed_blocks, depth, RS_LABELS, RS_TWIN),
        own_index & 1,
    )
    both_all, (keep_rows, send_rows) = all_gather_doubling(
        jnp.concatenate([text_half, image_half], 1),
        "dp",
        RS_ORDER[::-1],
        (keep_rows, send_rows),
        len(RS_ORDER) - 2,
    )
    text_all = both_all[:, :width]
    image_all = both_all[:, width:]

    logits, signs, coef = pair_coef(text_half, own_group, image_all, pair_group)
    caption_loss = -jnp.sum(jax.nn.log_sigmoid(signs * logits), 1) / total
    text_back = jnp.dot(coef, image_all, preferred_element_type=jnp.float32)
    _, _, coef_cols = pair_coef(image_half, own_group, text_all, pair_group)
    img_back = jnp.dot(coef_cols, text_all, preferred_element_type=jnp.float32)

    pooled_grad = (
        text_back - unit_text * jnp.sum(unit_text * text_back, 1, keepdims=True)
    ) * text_scale
    image_grad = (
        img_back - unit_image * jnp.sum(unit_image * img_back, 1, keepdims=True)
    ) * image_scale
    pooled_half = pooled_grad.astype(jnp.bfloat16)
    pooled_half, gbar_all = lax.optimization_barrier((pooled_half, gbar_all))
    hidden_grad = jnp.dot(pooled_half, w_down, preferred_element_type=jnp.float32)
    spread_grad = lax.dot_general(
        share_rows,
        hidden_grad,
        (((0,), (0,)), ((), ())),
        precision=lax.Precision.HIGHEST,
        preferred_element_type=jnp.float32,
    )
    pre_grad = (spread_grad * slope).astype(jnp.bfloat16)
    keep_term, send_term = [
        lax.dot_general(
            part, pre_grad, (((0,), (0,)), ((), ())), preferred_element_type=jnp.float32
        )
        for part in (keep_rows, send_rows)
    ]
    keep_term = lax.optimization_barrier(keep_term)
    pooled_rows = lax.all_to_all(
        pooled_half.reshape(captions, devices, rows), "dp", 1, 0
    ).reshape(total, rows)
    down_grad = lax.dot_general(
        pooled_rows, gbar_all, (((0,), (0,)), ((), ())), preferred_element_type=jnp.float32
    )
    up_grad, down_grad = reduce_scatter_halving(
        keep_term, send_term, "dp", RS_ORDER, RS_TWIN, down_grad, 1
    )
    return (caption_loss, image_grad, up_grad, down_grad)


def solution(mesh):
    in_specs = (P("dp", None), P("dp"), P("dp", None), P(), P(None, "mp"), P(None, "mp"))
    out_specs = (P("dp"), P("dp", None), P("dp", "mp"), P("dp", "mp"))
    return jax.shard_map(
        on_device, mesh=mesh, in_specs=in_specs, out_specs=out_specs, check_vma=False
    )
```

```python
import jax
import jax.numpy as jnp
from jax import lax
from jax.sharding import PartitionSpec as P

LOGIT_SCALE = 117.0
LOGIT_SHIFT = -12.9
RS_ORDER = (0, 3, 1, 4, 2, 5)
RS_TWIN = (0, 4, 3, 1, 5, 2)
RS_LABELS = (0, 5, 4, 3, 2, 1)


def passed_along(value, axis, steps):
    count = lax.axis_size(axis)
    pairs = [(source, (source + steps) % count) for source in range(count)]
    return lax.ppermute(value, axis, pairs)


def layer_norm(rows):
    center = rows - jnp.mean(rows, -1, keepdims=True)
    spread = jnp.mean(center * center, -1, keepdims=True)
    return center * lax.rsqrt(spread + 1e-06)


def gelu_pair(pre):
    const = 0.7978845608028654
    inner = const * (pre + 0.044715 * pre * pre * pre)
    tanh_u = jnp.tanh(inner)
    value = 0.5 * pre * (1.0 + tanh_u)
    slope = 0.5 * (1.0 + tanh_u) + 0.5 * pre * (1.0 - tanh_u * tanh_u) * const * (
        1.0 + 3.0 * 0.044715 * pre * pre
    )
    return (value, slope)


def unit_rows(rows):
    scale = lax.rsqrt(jnp.sum(rows * rows, 1, keepdims=True) + 1e-06)
    return (rows * scale, scale)


def pair_coef(own_rows, own_group, other_rows, other_group):
    logits = (
        LOGIT_SCALE
        * lax.dot_general(
            own_rows, other_rows, (((1,), (1,)), ((), ())), preferred_element_type=jnp.float32
        )
        + LOGIT_SHIFT
    )
    signs = jnp.where(own_group[:, None] == other_group[None, :], 1.0, -1.0).astype(jnp.float32)
    coef = (-LOGIT_SCALE * signs * jax.nn.sigmoid(-signs * logits)).astype(jnp.bfloat16)
    return (logits, signs, coef)


def permuted_blocks(blocks, depth, first, second):
    lead = blocks.shape[:1]
    swap = dict(zip(first, second))
    split = blocks.reshape(lead + (2,) * depth + blocks.shape[2:])
    moved = [1 + depth - 1 - swap[depth - 1 - place] for place in range(depth)]
    axes = [0] + moved + list(range(1 + depth, split.ndim))
    return jnp.transpose(split, axes).reshape(blocks.shape)


def first_stage_halves(natural, permuted, variant):
    shape = natural.shape
    halves = shape[:1] + (shape[1] // 2, 2) + shape[2:]
    own = jnp.where(variant == 0, natural, permuted).reshape(halves)
    other = jnp.where(variant == 0, permuted, natural).reshape(halves)
    keep = lax.dynamic_index_in_dim(own, variant, axis=2, keepdims=False)
    send = lax.dynamic_index_in_dim(other, 1 - variant, axis=2, keepdims=False)
    return (keep, send)


def reduce_scatter_halving(keep, send, axis, first, second, companion=None, tie_at=0):
    devices = lax.axis_size(axis)
    own_index = lax.axis_index(axis)
    pairs = [(source, source ^ 1) for source in range(devices)]
    state = keep + lax.ppermute(send, axis, pairs)
    variant = own_index & 1
    for step, (bit, twin) in enumerate(zip(first[1:], second[1:])):
        size = state.shape[0] // 2
        own_bit = jnp.where(variant == 0, (own_index >> bit) & 1, (own_index >> twin) & 1)
        keep = lax.dynamic_slice_in_dim(state, own_bit * size, size, axis=0)
        send = lax.dynamic_slice_in_dim(state, (1 - own_bit) * size, size, axis=0)
        pairs = [
            (source, source ^ (1 << (bit if source & 1 == 0 else twin)))
            for source in range(devices)
        ]
        received = lax.ppermute(send, axis, pairs)
        if step == tie_at and companion is not None:
            received, companion = lax.optimization_barrier((received, companion))
        state = keep + received
    return (state[0], companion)


def all_gather_doubling(block, axis, order, companion=None, tie_at=0):
    devices = lax.axis_size(axis)
    own_index = lax.axis_index(axis)
    depth = devices.bit_length() - 1
    state = block[None]
    gathered = []
    for step, bit in enumerate(order):
        place = sum(1 for done in gathered if done > bit)
        pairs = [(source, source ^ (1 << bit)) for source in range(devices)]
        other = lax.ppermute(state, axis, pairs)
        if step == tie_at and companion is not None:
            other, companion = lax.optimization_barrier((other, companion))
        low_first = jnp.stack([state, other], axis=place)
        high_first = jnp.stack([other, state], axis=place)
        state = jnp.where(((own_index >> bit) & 1) == 0, low_first, high_first)
        gathered.append(bit)
    return (state.reshape((devices * block.shape[0],) + block.shape[1:]), companion)


def on_device(tokens, lengths, images, pair_group, w_up, w_down):
    captions = lengths.shape[0]
    seq_len = tokens.shape[0] // captions
    width = tokens.shape[1]
    hidden = w_up.shape[1]
    devices = lax.axis_size("dp")
    own_index = lax.axis_index("dp")
    total = captions * devices
    rows = width // devices
    own_group = lax.dynamic_slice_in_dim(pair_group, own_index * captions, captions)

    unit_image, image_scale = unit_rows(images.astype(jnp.float32))
    image_half = unit_image.astype(jnp.bfloat16)

    tok_float = tokens.astype(jnp.float32)
    normed = layer_norm(tok_float).astype(jnp.bfloat16)
    pre = jnp.dot(normed, w_up, preferred_element_type=jnp.float32)
    value, slope = gelu_pair(pre)
    position = jnp.arange(seq_len, dtype=jnp.int32)
    valid = (position[None, :] < lengths[:, None]).astype(jnp.float32)
    share = valid / jnp.sum(valid, 1, keepdims=True)
    owner = jnp.arange(captions * seq_len, dtype=jnp.int32) // seq_len
    share_rows = jnp.where(
        owner[None, :] == jnp.arange(captions, dtype=jnp.int32)[:, None],
        share.reshape(1, captions * seq_len),
        0.0,
    )
    gmean = jnp.dot(
        share_rows, value, precision=lax.Precision.HIGHEST, preferred_element_type=jnp.float32
    )
    tmean = jnp.sum(tok_float.reshape(captions, seq_len, width) * share[:, :, None], 1)
    gbar = gmean.astype(jnp.bfloat16)
    gbar_all, _ = all_gather_doubling(gbar, "dp", RS_TWIN[::-1])
    partial_value = lax.dot_general(
        gbar, w_down, (((1,), (1,)), ((), ())), preferred_element_type=jnp.float32
    )
    pooled = tmean + (partial_value + passed_along(partial_value, "mp", 1))
    unit_text, text_scale = unit_rows(pooled)
    text_half = unit_text.astype(jnp.bfloat16)
    normed_late, pooled = lax.optimization_barrier((normed, pooled))
    normed_blocks = normed_late.reshape(captions * seq_len, devices, rows)
    depth = devices.bit_length() - 1
    keep_rows, send_rows = first_stage_halves(
        permuted_blocks(normed_blocks, depth, RS_LABELS, RS_ORDER),
        permuted_blocks(normed_blocks, depth, RS_LABELS, RS_TWIN),
        own_index & 1,
    )
    both_all, (keep_rows, send_rows) = all_gather_doubling(
        jnp.concatenate([text_half, image_half], 1),
        "dp",
        RS_ORDER[::-1],
        (keep_rows, send_rows),
        len(RS_ORDER) - 2,
    )
    text_all = both_all[:, :width]
    image_all = both_all[:, width:]

    logits, signs, coef = pair_coef(text_half, own_group, image_all, pair_group)
    caption_loss = -jnp.sum(jax.nn.log_sigmoid(signs * logits), 1) / total
    text_back = jnp.dot(coef, image_all, preferred_element_type=jnp.float32)
    _, _, coef_cols = pair_coef(image_half, own_group, text_all, pair_group)
    img_back = jnp.dot(coef_cols, text_all, preferred_element_type=jnp.float32)

    pooled_grad = (
        text_back - unit_text * jnp.sum(unit_text * text_back, 1, keepdims=True)
    ) * text_scale
    image_grad = (
        img_back - unit_image * jnp.sum(unit_image * img_back, 1, keepdims=True)
    ) * image_scale
    pooled_half = pooled_grad.astype(jnp.bfloat16)
    pooled_half, gbar_all = lax.optimization_barrier((pooled_half, gbar_all))
    hidden_grad = jnp.dot(pooled_half, w_down, preferred_element_type=jnp.float32)
    spread_grad = lax.dot_general(
        share_rows,
        hidden_grad,
        (((0,), (0,)), ((), ())),
        precision=lax.Precision.HIGHEST,
        preferred_element_type=jnp.float32,
    )
    pre_grad = (spread_grad * slope).astype(jnp.bfloat16)
    keep_term, send_term = [
        lax.dot_general(
            part, pre_grad, (((0,), (0,)), ((), ())), preferred_element_type=jnp.float32
        )
        for part in (keep_rows, send_rows)
    ]
    keep_term = lax.optimization_barrier(keep_term)
    pooled_rows = lax.all_to_all(
        pooled_half.reshape(captions, devices, rows), "dp", 1, 0
    ).reshape(total, rows)
    down_grad = lax.dot_general(
        pooled_rows, gbar_all, (((0,), (0,)), ((), ())), preferred_element_type=jnp.float32
    )
    up_grad, down_grad = reduce_scatter_halving(
        keep_term, send_term, "dp", RS_ORDER, RS_TWIN, down_grad, 3
    )
    return (caption_loss, image_grad, up_grad, down_grad)


def solution(mesh):
    in_specs = (P("dp", None), P("dp"), P("dp", None), P(), P(None, "mp"), P(None, "mp"))
    out_specs = (P("dp"), P("dp", None), P("dp", "mp"), P("dp", "mp"))
    return jax.shard_map(
        on_device, mesh=mesh, in_specs=in_specs, out_specs=out_specs, check_vma=False
    )
```
